256 devices in a mesh: req: 32 (over y, z), tp: 8 (over x, core).
Axes of the slice: x: 4, y: 4, z: 8, core: 2. Of those that a mesh axis runs over, the one named last changes fastest.
Arguments:
- tokens: bfloat16 [32768, 1792], P(('req', 'tp')), may hold values from -6 to 6
- norm_gain: float32 [1792], replicated, may hold values from 0.25 to 1.75
- ffn_gain: float32 [1792], replicated, may hold values from 0.25 to 1.75
- mix_weight: bfloat16 [1792, 4, 1792], P('req', None, 'tp'), may hold values from -0.125 to 0.125
- out_weight: bfloat16 [1792, 1792], P('tp', 'req'), may hold values from -0.125 to 0.125
- ffn_weight: bfloat16 [1792, 2, 7168], P('req', None, 'tp'), may hold values from -0.125 to 0.125
- down_weight: bfloat16 [7168, 1792], P('tp', 'req'), may hold values from -0.0625 to 0.0625
- conv_taps: float32 [3, 1792], P(None, 'tp'), may hold values from -3 to 3
- past_cache: bfloat16 [32, 2, 64, 1792], P('req', None, None, 'tp'), may hold values from -210 to 210
- cached_len: int32 [32], P('req'), may hold values from 0 to 8192, as said below
Outputs:
- layer_out: bfloat16 [32768, 1792], P(('req', 'tp'))
- new_cache: bfloat16 [32, 2, 64, 1792], P('req', None, None, 'tp')
The draws below stay inside these ranges and needn't reach their ends.
Inputs may be any that keep to these rules, and one draw needn't show every extreme that they name: `cached_len`: one request has exactly 8192 cached positions and another fewer than 64.
All inputs are finite; a program needn't handle non-finite values.
Results may differ from the reference program's by a relative error of at most 0.02.
Values may be sent and summed in bfloat16 or wider, within the bound.
No kernel may reach another device: no remote copies, remote signals or barrier semaphores. Data moves between devices by JAX's collectives and lax.ppermute only.
A program may use at most 64 MiB of HBM per device.

```python
import math
import jax
import jax.numpy as jnp
from jax import lax

D = 1792
HD = 112
FF_WIN = 7168
WIN = 64
KCONV = 3
MAXLEN = 8192
SPAN = 1024
REQS = 32
TOKENS = 32768
N_TP = 8


def draw_cached_len(key, part):
    keys_list = jax.random.split(key, 5)
    left_draw = jax.random.randint(keys_list[0], (REQS,), 0, MAXLEN + 1)
    right_draw = jax.random.randint(keys_list[1], (REQS,), 0, MAXLEN + 1)
    lengths = left_draw * right_draw // MAXLEN
    top_slot = jax.random.randint(keys_list[2], (), 0, REQS)
    low_slot = (top_slot + 1 + jax.random.randint(keys_list[3], (), 0, REQS - 1)) % REQS
    low_value = jax.random.randint(keys_list[4], (), 0, WIN)
    request_ids = jnp.arange(REQS)
    lengths = jnp.where(request_ids == top_slot, MAXLEN, lengths)
    lengths = jnp.where(request_ids == low_slot, low_value, lengths)
    return lengths.astype(jnp.int32)


def draw_past_cache(key, part):
    keys_list = jax.random.split(jax.random.fold_in(key, 11), 1)
    values = jax.random.normal(keys_list[0], (REQS, 2, WIN, D), jnp.float32)
    return values.astype(jnp.bfloat16)


def block_scale(stream_key, shape, pieces, low, high):
    loudness, own = 1.0, jax.random.fold_in(stream_key, 6)
    for position, blocks in pieces:
        steps = jnp.exp(jax.random.uniform(jax.random.fold_in(own, position), (blocks,), jnp.float32, low / len(pieces), high / len(pieces)))
        loudness = loudness * jnp.repeat(steps, shape[position] // blocks).reshape([-1 if axis == position else 1 for axis in range(len(shape))])
    return loudness


def centred(stream_key, shape, scale, reach, pieces=(), kind=jnp.bfloat16):
    array = jax.random.normal(stream_key, shape, jnp.float32) * scale
    if len(pieces) > 0:
        array = block_scale(stream_key, shape, pieces, -0.22, 0.18) * array
    return jnp.clip(array, min=-reach, max=reach).astype(kind)


def setup_inputs(seed: int = 0) -> dict:
    seeds = jax.random.split(jax.random.key(seed), 11)
    return {
        "tokens": centred(seeds[0], (TOKENS, D), 1.0, 6.0, ((0, 256),)),
        "norm_gain": jnp.clip(1.0 + 0.15 * jax.random.normal(seeds[1], (D,), jnp.float32), 0.25, 1.75),
        "ffn_gain": jnp.clip(1.0 + 0.15 * jax.random.normal(seeds[2], (D,), jnp.float32), 0.25, 1.75),
        "mix_weight": centred(seeds[3], (D, 4, D), D ** -0.5, 0.125, ((0, 32), (2, 8))),
        "out_weight": centred(seeds[4], (D, D), D ** -0.5, 0.125, ((0, 8), (1, 32))),
        "ffn_weight": centred(seeds[5], (D, 2, FF_WIN), D ** -0.5, 0.125, ((0, 32), (2, 8))),
        "down_weight": centred(seeds[6], (FF_WIN, D), FF_WIN ** -0.5, 0.0625, ((0, 8), (1, 32))),
        "conv_taps": centred(seeds[7], (KCONV, D), 0.6, 3.0, ((1, 8),), jnp.float32),
        "past_cache": draw_past_cache(jax.random.fold_in(seeds[10], 71), 0),
        "cached_len": draw_cached_len(jax.random.fold_in(seeds[10], 71), 0),
    }


def normed(row_vals, gain):
    floats = row_vals.astype(jnp.float32)
    scaled = floats * lax.rsqrt(lax.optimization_barrier(jnp.mean(floats * floats, axis=-1, keepdims=True)) + 1e-05)
    return (scaled * gain.astype(jnp.float32)).astype(jnp.bfloat16)

def window_attend(queries, key_rows, value_rows, length, window):
    row_count, head_count, head_size = queries.shape
    block_rows = min(512, row_count)
    score_scale = 1.0 / math.sqrt(head_size)

    def one_block(block_index):
        begin_row = block_index * block_rows
        query_block = lax.dynamic_slice_in_dim(queries, begin_row, block_rows, 0)
        key_block = lax.dynamic_slice_in_dim(key_rows, begin_row, block_rows + window, 0)
        value_block = lax.dynamic_slice_in_dim(value_rows, begin_row, block_rows + window, 0)
        scores = jnp.einsum('qhd,khd->hqk', query_block.astype(jnp.float32), key_block.astype(jnp.float32)) * score_scale
        row_ids = begin_row + jnp.arange(block_rows, dtype=jnp.int32)[:, None]
        col_ids = begin_row + jnp.arange(block_rows + window, dtype=jnp.int32)[None, :]
        usable = (col_ids > row_ids) & (col_ids <= row_ids + window) & (col_ids >= window - length)
        scores = jnp.where(usable[None], scores, -1e+30)
        row_max = lax.optimization_barrier(jnp.max(scores, axis=-1, keepdims=True))
        exponent = jnp.exp(scores - row_max)
        weights = (exponent / lax.optimization_barrier(jnp.sum(exponent, axis=-1, keepdims=True))).astype(jnp.bfloat16)
        return jnp.einsum('hqk,khd->qhd', weights.astype(jnp.float32), value_block.astype(jnp.float32))
    blocks = lax.map(one_block, jnp.arange(row_count // block_rows, dtype=jnp.int32))
    return blocks.reshape(row_count, head_count, head_size)

def mix_request(projected, cache_rows, length, tap_table, window, head_size):
    row_count, feat_width = (projected.shape[0], projected.shape[2])
    time_order = (length + jnp.arange(window, dtype=jnp.int32)) % window
    earlier = cache_rows[:, time_order]
    key_rows = jnp.concatenate([earlier[0], projected[:, 1]], axis=0)
    value_rows = jnp.concatenate([earlier[1], projected[:, 2]], axis=0)
    head_count = feat_width // head_size
    attended = window_attend(projected[:, 0].reshape(row_count, head_count, head_size), key_rows.reshape(-1, head_count, head_size), value_rows.reshape(-1, head_count, head_size), length, window).reshape(row_count, feat_width)
    positions = jnp.arange(window + row_count, dtype=jnp.int32)
    alive_mask = (positions >= window - length)[:, None]
    masked_values = jnp.where(alive_mask, value_rows.astype(jnp.float32), jnp.float32(0.0))
    tap_count = tap_table.shape[0]
    convolved = jnp.zeros((row_count, feat_width), jnp.float32)
    for tap_index in range(tap_count):
        begin_row = window - (tap_count - 1) + tap_index
        convolved = convolved + tap_table[tap_index].astype(jnp.float32) * masked_values[begin_row:begin_row + row_count]
    mixed_heads = (attended + projected[:, 3].astype(jnp.float32) * convolved).astype(jnp.bfloat16)
    slot_source = row_count - window + (jnp.arange(window, dtype=jnp.int32) - length - row_count) % window
    renewed = jnp.stack([projected[:, 1], projected[:, 2]])[:, slot_source]
    return (mixed_heads, renewed)

def reference(tokens, norm_gain, ffn_gain, mix_weight, out_weight, ffn_weight, down_weight, conv_taps, past_cache, cached_len):
    feat_group = D // N_TP
    ffn_group = FF_WIN // N_TP

    def one_request(items):
        token_rows, cache_rows, length = items
        normed_in = normed(token_rows, norm_gain)
        projected = jnp.dot(normed_in, mix_weight.reshape(D, 4 * D), preferred_element_type=jnp.float32)
        projected = projected.astype(jnp.bfloat16).reshape(SPAN, 4, D)
        mixed_heads, renewed = mix_request(projected, cache_rows, length, conv_taps, WIN, HD)
        attn_sum = jnp.zeros((SPAN, D), jnp.float32)
        for group_id in range(N_TP):
            group_begin = group_id * feat_group
            term_rows = jnp.dot(mixed_heads[:, group_begin:group_begin + feat_group], out_weight[group_begin:group_begin + feat_group], preferred_element_type=jnp.float32).astype(jnp.bfloat16)
            attn_sum = attn_sum + lax.optimization_barrier(term_rows).astype(jnp.float32)
        residual = (token_rows.astype(jnp.float32) + attn_sum).astype(jnp.bfloat16)
        ffn_in = normed(residual, ffn_gain)
        gate_up = jnp.dot(ffn_in, ffn_weight.reshape(D, 2 * FF_WIN), preferred_element_type=jnp.float32)
        activated = (jax.nn.silu(gate_up[:, :FF_WIN]) * gate_up[:, FF_WIN:]).astype(jnp.bfloat16)
        ffn_sum = jnp.zeros((SPAN, D), jnp.float32)
        for group_id in range(N_TP):
            group_begin = group_id * ffn_group
            term_rows = jnp.dot(activated[:, group_begin:group_begin + ffn_group], down_weight[group_begin:group_begin + ffn_group], preferred_element_type=jnp.float32).astype(jnp.bfloat16)
            ffn_sum = ffn_sum + lax.optimization_barrier(term_rows).astype(jnp.float32)
        layer_out = (residual.astype(jnp.float32) + ffn_sum).astype(jnp.bfloat16)
        return (layer_out, renewed)
    layer_out, new_cache = lax.map(one_request, (tokens.reshape(REQS, SPAN, D), past_cache, cached_len))
    return (layer_out.reshape(TOKENS, D), new_cache)
```

```python
import math

import jax
import jax.numpy as jnp
from jax import lax
from jax.sharding import PartitionSpec as P

HD = 112
WIN = 64


def normed(row_vals, gain):
    floats = row_vals.astype(jnp.float32)
    scaled = floats * lax.rsqrt(jnp.mean(floats * floats, axis=-1, keepdims=True) + 1e-05)
    return (scaled * gain).astype(jnp.bfloat16)


def window_attend(queries, key_rows, value_rows, length, window):
    row_count, head_count, head_size = queries.shape
    nb = row_count // window
    score_scale = 1.0 / math.sqrt(head_size)
    qb = queries.reshape(nb, window, head_count, head_size)

    def blocks(rows):
        lo = rows[:row_count].reshape(nb, window, head_count, head_size)
        hi = rows[window:].reshape(nb, window, head_count, head_size)
        return jnp.concatenate([lo, hi], axis=1)

    kb = blocks(key_rows)
    vb = blocks(value_rows)
    scores = (
        jnp.einsum("bqhd,bkhd->bhqk", qb, kb, preferred_element_type=jnp.float32) * score_scale
    )
    i = jnp.arange(window, dtype=jnp.int32)[:, None]
    j = jnp.arange(2 * window, dtype=jnp.int32)[None, :]
    b = jnp.arange(nb, dtype=jnp.int32)[:, None, None]
    usable = (j > i)[None] & (j <= i + window)[None] & (b * window + j >= window - length)
    scores = jnp.where(usable[:, None], scores, -1e30)
    row_max = jnp.max(scores, axis=-1, keepdims=True)
    exponent = jnp.exp(scores - row_max)
    weights = (exponent / jnp.sum(exponent, axis=-1, keepdims=True)).astype(jnp.bfloat16)
    out = jnp.einsum("bhqk,bkhd->bqhd", weights, vb, preferred_element_type=jnp.float32)
    return out.reshape(row_count, head_count, head_size)


def mix_request(projected, cache_rows, length, tap_table, window, head_size):
    row_count, feat_width = (projected.shape[0], projected.shape[2])
    time_order = (length + jnp.arange(window, dtype=jnp.int32)) % window
    earlier = cache_rows[:, time_order]
    key_rows = jnp.concatenate([earlier[0], projected[:, 1]], axis=0)
    value_rows = jnp.concatenate([earlier[1], projected[:, 2]], axis=0)
    head_count = feat_width // head_size
    attended = window_attend(
        projected[:, 0].reshape(row_count, head_count, head_size),
        key_rows.reshape(-1, head_count, head_size),
        value_rows.reshape(-1, head_count, head_size),
        length,
        window,
    ).reshape(row_count, feat_width)
    positions = jnp.arange(window + row_count, dtype=jnp.int32)
    alive_mask = (positions >= window - length)[:, None]
    masked_values = jnp.where(alive_mask, value_rows.astype(jnp.float32), jnp.float32(0.0))
    tap_count = tap_table.shape[0]
    convolved = jnp.zeros((row_count, feat_width), jnp.float32)
    for tap_index in range(tap_count):
        begin_row = window - (tap_count - 1) + tap_index
        convolved = (
            convolved + tap_table[tap_index] * masked_values[begin_row : begin_row + row_count]
        )
    mixed_heads = (attended + projected[:, 3].astype(jnp.float32) * convolved).astype(jnp.bfloat16)
    slot_source = (
        row_count - window + (jnp.arange(window, dtype=jnp.int32) - length - row_count) % window
    )
    renewed = jnp.stack([projected[:, 1], projected[:, 2]])[:, slot_source]
    return (mixed_heads, renewed)


def gather_weights(mix_weight, out_weight, ffn_weight, down_weight):
    rows = mix_weight.shape[0]
    pieces = [
        mix_weight.reshape(rows, -1),
        ffn_weight.reshape(rows, -1),
        down_weight.T,
        out_weight.T,
    ]
    widths = [p.shape[1] for p in pieces]
    got = lax.all_gather(jnp.concatenate(pieces, axis=1), "req", axis=0, tiled=True)
    parts = []
    start = 0
    for w in widths:
        parts.append(got[:, start : start + w])
        start += w
    return parts


def tp_gather(x):
    n = lax.axis_size("tp")
    return lax.all_to_all(jnp.tile(x, (n, 1)), "tp", 0, 0, tiled=True)


def tp_sum_scatter(x):
    n = lax.axis_size("tp")
    got = lax.all_to_all(x, "tp", 0, 0, tiled=True)
    return got.reshape((n, -1) + x.shape[1:]).astype(jnp.float32).sum(axis=0)


def local(
    tokens,
    norm_gain,
    ffn_gain,
    mix_weight,
    out_weight,
    ffn_weight,
    down_weight,
    conv_taps,
    past_cache,
    cached_len,
):
    feat_width = mix_weight.shape[2]
    ffn_width = ffn_weight.shape[2]
    mix_all, ffn_all, down_t, out_t = gather_weights(mix_weight, out_weight, ffn_weight, down_weight)
    normed_all = tp_gather(normed(tokens, norm_gain))
    row_total = normed_all.shape[0]
    projected = jnp.dot(normed_all, mix_all, preferred_element_type=jnp.float32)
    projected = projected.astype(jnp.bfloat16).reshape(row_total, 4, feat_width)
    mixed_heads, renewed = mix_request(projected, past_cache[0], cached_len[0], conv_taps, WIN, HD)
    attn_full = lax.dot_general(
        mixed_heads, out_t, (((1,), (1,)), ((), ())), preferred_element_type=jnp.float32
    )
    attn_part = tp_sum_scatter(attn_full.astype(jnp.bfloat16))
    residual = (tokens.astype(jnp.float32) + attn_part).astype(jnp.bfloat16)
    ffn_in = tp_gather(normed(residual, ffn_gain))
    gate_up = jnp.dot(ffn_in, ffn_all, preferred_element_type=jnp.float32)
    activated = (jax.nn.silu(gate_up[:, :ffn_width]) * gate_up[:, ffn_width:]).astype(jnp.bfloat16)
    ffn_full = lax.dot_general(
        activated, down_t, (((1,), (1,)), ((), ())), preferred_element_type=jnp.float32
    )
    ffn_part = tp_sum_scatter(ffn_full.astype(jnp.bfloat16))
    layer_out = (residual.astype(jnp.float32) + ffn_part).astype(jnp.bfloat16)
    return (layer_out, renewed[None])


def solution(mesh):
    in_specs = (
        P(("req", "tp"), None),
        P(),
        P(),
        P("req", None, "tp"),
        P("tp", "req"),
        P("req", None, "tp"),
        P("tp", "req"),
        P(None, "tp"),
        P("req", None, None, "tp"),
        P("req"),
    )
    out_specs = (P(("req", "tp"), None), P("req", None, None, "tp"))
    return jax.shard_map(local, mesh=mesh, in_specs=in_specs, out_specs=out_specs, check_vma=False)
```

```python
import math

import jax
import jax.numpy as jnp
from jax import lax
from jax.sharding import PartitionSpec as P

HD = 112
WIN = 64


def normed(row_vals, gain):
    floats = row_vals.astype(jnp.float32)
    scaled = floats * lax.rsqrt(jnp.mean(floats * floats, axis=-1, keepdims=True) + 1e-05)
    return (scaled * gain).astype(jnp.bfloat16)


def window_attend(queries, key_rows, value_rows, length, window):
    row_count, head_count, head_size = queries.shape
    nb = row_count // window
    score_scale = 1.0 / math.sqrt(head_size)
    qb = queries.reshape(nb, window, head_count, head_size)

    def blocks(rows):
        lo = rows[:row_count].reshape(nb, window, head_count, head_size)
        hi = rows[window:].reshape(nb, window, head_count, head_size)
        return jnp.concatenate([lo, hi], axis=1)

    kb = blocks(key_rows)
    vb = blocks(value_rows)
    scores = (
        jnp.einsum("bqhd,bkhd->bhqk", qb, kb, preferred_element_type=jnp.float32) * score_scale
    )
    i = jnp.arange(window, dtype=jnp.int32)[:, None]
    j = jnp.arange(2 * window, dtype=jnp.int32)[None, :]
    b = jnp.arange(nb, dtype=jnp.int32)[:, None, None]
    usable = (j > i)[None] & (j <= i + window)[None] & (b * window + j >= window - length)
    scores = jnp.where(usable[:, None], scores, -1e30)
    row_max = jnp.max(scores, axis=-1, keepdims=True)
    exponent = jnp.exp(scores - row_max)
    weights = (exponent / jnp.sum(exponent, axis=-1, keepdims=True)).astype(jnp.bfloat16)
    out = jnp.einsum("bhqk,bkhd->bqhd", weights, vb, preferred_element_type=jnp.float32)
    return out.reshape(row_count, head_count, head_size)


def mix_request(projected, cache_rows, length, tap_table, window, head_size):
    row_count, feat_width = (projected.shape[0], projected.shape[2])
    time_order = (length + jnp.arange(window, dtype=jnp.int32)) % window
    earlier = cache_rows[:, time_order]
    key_rows = jnp.concatenate([earlier[0], projected[:, 1]], axis=0)
    value_rows = jnp.concatenate([earlier[1], projected[:, 2]], axis=0)
    head_count = feat_width // head_size
    attended = window_attend(
        projected[:, 0].reshape(row_count, head_count, head_size),
        key_rows.reshape(-1, head_count, head_size),
        value_rows.reshape(-1, head_count, head_size),
        length,
        window,
    ).reshape(row_count, feat_width)
    positions = jnp.arange(window + row_count, dtype=jnp.int32)
    alive_mask = (positions >= window - length)[:, None]
    masked_values = jnp.where(alive_mask, value_rows.astype(jnp.float32), jnp.float32(0.0))
    tap_count = tap_table.shape[0]
    convolved = jnp.zeros((row_count, feat_width), jnp.float32)
    for tap_index in range(tap_count):
        begin_row = window - (tap_count - 1) + tap_index
        convolved = (
            convolved + tap_table[tap_index] * masked_values[begin_row : begin_row + row_count]
        )
    mixed_heads = (attended + projected[:, 3].astype(jnp.float32) * convolved).astype(jnp.bfloat16)
    slot_source = (
        row_count - window + (jnp.arange(window, dtype=jnp.int32) - length - row_count) % window
    )
    renewed = jnp.stack([projected[:, 1], projected[:, 2]])[:, slot_source]
    return (mixed_heads, renewed)


def gather_packed(pieces):
    widths = [p.shape[1] for p in pieces]
    got = lax.all_gather(jnp.concatenate(pieces, axis=1), "req", axis=0, tiled=True)
    parts = []
    start = 0
    for w in widths:
        parts.append(got[:, start : start + w])
        start += w
    return parts


def tp_gather(x):
    n = lax.axis_size("tp")
    return lax.all_to_all(jnp.tile(x, (n, 1)), "tp", 0, 0, tiled=True)


def tp_sum_scatter(x):
    n = lax.axis_size("tp")
    got = lax.all_to_all(x, "tp", 0, 0, tiled=True)
    return got.reshape((n, -1) + x.shape[1:]).astype(jnp.float32).sum(axis=0)


def local(
    tokens,
    norm_gain,
    ffn_gain,
    mix_weight,
    out_weight,
    ffn_weight,
    down_weight,
    conv_taps,
    past_cache,
    cached_len,
):
    feat_width = mix_weight.shape[2]
    ffn_width = ffn_weight.shape[2]
    rows = mix_weight.shape[0]
    mix_all, out_t = gather_packed([mix_weight.reshape(rows, -1), out_weight.T])
    ffn_all, down_t = gather_packed([ffn_weight.reshape(rows, -1), down_weight.T])
    normed_all = tp_gather(normed(tokens, norm_gain))
    row_total = normed_all.shape[0]
    projected = jnp.dot(normed_all, mix_all, preferred_element_type=jnp.float32)
    projected = projected.astype(jnp.bfloat16).reshape(row_total, 4, feat_width)
    mixed_heads, renewed = mix_request(projected, past_cache[0], cached_len[0], conv_taps, WIN, HD)
    attn_full = lax.dot_general(
        mixed_heads, out_t, (((1,), (1,)), ((), ())), preferred_element_type=jnp.float32
    )
    attn_part = tp_sum_scatter(attn_full.astype(jnp.bfloat16))
    residual = (tokens.astype(jnp.float32) + attn_part).astype(jnp.bfloat16)
    ffn_in = tp_gather(normed(residual, ffn_gain))
    gate_up = jnp.dot(ffn_in, ffn_all, preferred_element_type=jnp.float32)
    activated = (jax.nn.silu(gate_up[:, :ffn_width]) * gate_up[:, ffn_width:]).astype(jnp.bfloat16)
    ffn_full = lax.dot_general(
        activated, down_t, (((1,), (1,)), ((), ())), preferred_element_type=jnp.float32
    )
    ffn_part = tp_sum_scatter(ffn_full.astype(jnp.bfloat16))
    layer_out = (residual.astype(jnp.float32) + ffn_part).astype(jnp.bfloat16)
    return (layer_out, renewed[None])


def solution(mesh):
    in_specs = (
        P(("req", "tp"), None),
        P(),
        P(),
        P("req", None, "tp"),
        P("tp", "req"),
        P("req", None, "tp"),
        P("tp", "req"),
        P(None, "tp"),
        P("req", None, None, "tp"),
        P("req"),
    )
    out_specs = (P(("req", "tp"), None), P("req", None, None, "tp"))
    return jax.shard_map(local, mesh=mesh, in_specs=in_specs, out_specs=out_specs, check_vma=False)
```

```python
import math

import jax
import jax.numpy as jnp
from jax import lax
from jax.sharding import PartitionSpec as P

HD = 112
WIN = 64


def normed(row_vals, gain):
    floats = row_vals.astype(jnp.float32)
    scaled = floats * lax.rsqrt(jnp.mean(floats * floats, axis=-1, keepdims=True) + 1e-05)
    return (scaled * gain).astype(jnp.bfloat16)


def window_attend(queries, key_rows, value_rows, length, window):
    row_count, head_count, head_size = queries.shape
    nb = row_count // window
    score_scale = 1.0 / math.sqrt(head_size)
    qb = queries.reshape(nb, window, head_count, head_size)

    def blocks(rows):
        lo = rows[:row_count].reshape(nb, window, head_count, head_size)
        hi = rows[window:].reshape(nb, window, head_count, head_size)
        return jnp.concatenate([lo, hi], axis=1)

    kb = blocks(key_rows)
    vb = blocks(value_rows)
    scores = (
        jnp.einsum("bqhd,bkhd->bhqk", qb, kb, preferred_element_type=jnp.float32) * score_scale
    )
    i = jnp.arange(window, dtype=jnp.int32)[:, None]
    j = jnp.arange(2 * window, dtype=jnp.int32)[None, :]
    b = jnp.arange(nb, dtype=jnp.int32)[:, None, None]
    usable = (j > i)[None] & (j <= i + window)[None] & (b * window + j >= window - length)
    scores = jnp.where(usable[:, None], scores, -1e30)
    row_max = jnp.max(scores, axis=-1, keepdims=True)
    exponent = jnp.exp(scores - row_max)
    weights = (exponent / jnp.sum(exponent, axis=-1, keepdims=True)).astype(jnp.bfloat16)
    out = jnp.einsum("bhqk,bkhd->bqhd", weights, vb, preferred_element_type=jnp.float32)
    return out.reshape(row_count, head_count, head_size)


def mix_request(projected, cache_rows, length, tap_table, window, head_size):
    row_count, feat_width = (projected.shape[0], projected.shape[2])
    time_order = (length + jnp.arange(window, dtype=jnp.int32)) % window
    earlier = cache_rows[:, time_order]
    key_rows = jnp.concatenate([earlier[0], projected[:, 1]], axis=0)
    value_rows = jnp.concatenate([earlier[1], projected[:, 2]], axis=0)
    head_count = feat_width // head_size
    attended = window_attend(
        projected[:, 0].reshape(row_count, head_count, head_size),
        key_rows.reshape(-1, head_count, head_size),
        value_rows.reshape(-1, head_count, head_size),
        length,
        window,
    ).reshape(row_count, feat_width)
    positions = jnp.arange(window + row_count, dtype=jnp.int32)
    alive_mask = (positions >= window - length)[:, None]
    masked_values = jnp.where(alive_mask, value_rows.astype(jnp.float32), jnp.float32(0.0))
    tap_count = tap_table.shape[0]
    convolved = jnp.zeros((row_count, feat_width), jnp.float32)
    for tap_index in range(tap_count):
        begin_row = window - (tap_count - 1) + tap_index
        convolved = (
            convolved + tap_table[tap_index] * masked_values[begin_row : begin_row + row_count]
        )
    mixed_heads = (attended + projected[:, 3].astype(jnp.float32) * convolved).astype(jnp.bfloat16)
    slot_source = (
        row_count - window + (jnp.arange(window, dtype=jnp.int32) - length - row_count) % window
    )
    renewed = jnp.stack([projected[:, 1], projected[:, 2]])[:, slot_source]
    return (mixed_heads, renewed)


def gather_packed(pieces):
    widths = [p.shape[1] for p in pieces]
    got = lax.all_gather(jnp.concatenate(pieces, axis=1), "req", axis=0, tiled=True)
    parts = []
    start = 0
    for w in widths:
        parts.append(got[:, start : start + w])
        start += w
    return parts


def tp_gather(x):
    nx = lax.axis_size("tpx")
    nc = lax.axis_size("tpc")
    by_chip = lax.all_to_all(jnp.tile(x[None], (nx, 1, 1)), "tpx", 0, 0, tiled=True)
    both = jnp.broadcast_to(by_chip[:, None], (nx, nc) + x.shape)
    got = lax.all_to_all(both, "tpc", 1, 1, tiled=True)
    return got.reshape((nx * nc * x.shape[0],) + x.shape[1:])


def tp_sum_scatter(x):
    nx = lax.axis_size("tpx")
    nc = lax.axis_size("tpc")
    rows = x.shape[0] // (nx * nc)
    parts = x.reshape((nx, nc, rows) + x.shape[1:])
    pair = lax.all_to_all(parts, "tpc", 1, 1, tiled=True)
    pair = pair.astype(jnp.float32).sum(axis=1).astype(jnp.bfloat16)
    chips = lax.all_to_all(pair, "tpx", 0, 0, tiled=True)
    return chips.astype(jnp.float32).sum(axis=0)


def local(
    tokens,
    norm_gain,
    ffn_gain,
    mix_weight,
    out_weight,
    ffn_weight,
    down_weight,
    conv_taps,
    past_cache,
    cached_len,
):
    feat_width = mix_weight.shape[2]
    ffn_width = ffn_weight.shape[2]
    rows = mix_weight.shape[0]
    mix_all, out_t = gather_packed([mix_weight.reshape(rows, -1), out_weight.T])
    ffn_all, down_t = gather_packed([ffn_weight.reshape(rows, -1), down_weight.T])
    normed_all = tp_gather(normed(tokens, norm_gain))
    row_total = normed_all.shape[0]
    projected = jnp.dot(normed_all, mix_all, preferred_element_type=jnp.float32)
    projected = projected.astype(jnp.bfloat16).reshape(row_total, 4, feat_width)
    mixed_heads, renewed = mix_request(projected, past_cache[0], cached_len[0], conv_taps, WIN, HD)
    attn_full = lax.dot_general(
        mixed_heads, out_t, (((1,), (1,)), ((), ())), preferred_element_type=jnp.float32
    )
    attn_part = tp_sum_scatter(attn_full.astype(jnp.bfloat16))
    residual = (tokens.astype(jnp.float32) + attn_part).astype(jnp.bfloat16)
    ffn_in = tp_gather(normed(residual, ffn_gain))
    gate_up = jnp.dot(ffn_in, ffn_all, preferred_element_type=jnp.float32)
    activated = (jax.nn.silu(gate_up[:, :ffn_width]) * gate_up[:, ffn_width:]).astype(jnp.bfloat16)
    ffn_full = lax.dot_general(
        activated, down_t, (((1,), (1,)), ((), ())), preferred_element_type=jnp.float32
    )
    ffn_part = tp_sum_scatter(ffn_full.astype(jnp.bfloat16))
    layer_out = (residual.astype(jnp.float32) + ffn_part).astype(jnp.bfloat16)
    return (layer_out, renewed[None])


def solution(mesh):
    n_req, n_tp = mesh.devices.shape
    split = jax.sharding.Mesh(mesh.devices.reshape(n_req, n_tp // 2, 2), ("req", "tpx", "tpc"))
    tp = ("tpx", "tpc")
    in_specs = (
        P(("req",) + tp, None),
        P(),
        P(),
        P("req", None, tp),
        P(tp, "req"),
        P("req", None, tp),
        P(tp, "req"),
        P(None, tp),
        P("req", None, None, tp),
        P("req"),
    )
    out_specs = (P(("req",) + tp, None), P("req", None, None, tp))
    return jax.shard_map(local, mesh=split, in_specs=in_specs, out_specs=out_specs, check_vma=False)
```

```python
import math

import jax
import jax.numpy as jnp
from jax import lax
from jax.sharding import PartitionSpec as P

HD = 112
WIN = 64
REQ = ("ry", "rz")


def normed(row_vals, gain):
    floats = row_vals.astype(jnp.float32)
    scaled = floats * lax.rsqrt(jnp.mean(floats * floats, axis=-1, keepdims=True) + 1e-05)
    return (scaled * gain).astype(jnp.bfloat16)


def window_attend(queries, key_rows, value_rows, length, window):
    row_count, head_count, head_size = queries.shape
    nb = row_count // window
    score_scale = 1.0 / math.sqrt(head_size)
    qb = queries.reshape(nb, window, head_count, head_size)

    def blocks(rows):
        lo = rows[:row_count].reshape(nb, window, head_count, head_size)
        hi = rows[window:].reshape(nb, window, head_count, head_size)
        return jnp.concatenate([lo, hi], axis=1)

    kb = blocks(key_rows)
    vb = blocks(value_rows)
    scores = (
        jnp.einsum("bqhd,bkhd->bhqk", qb, kb, preferred_element_type=jnp.float32) * score_scale
    )
    i = jnp.arange(window, dtype=jnp.int32)[:, None]
    j = jnp.arange(2 * window, dtype=jnp.int32)[None, :]
    b = jnp.arange(nb, dtype=jnp.int32)[:, None, None]
    usable = (j > i)[None] & (j <= i + window)[None] & (b * window + j >= window - length)
    scores = jnp.where(usable[:, None], scores, -1e30)
    row_max = jnp.max(scores, axis=-1, keepdims=True)
    exponent = jnp.exp(scores - row_max)
    weights = (exponent / jnp.sum(exponent, axis=-1, keepdims=True)).astype(jnp.bfloat16)
    out = jnp.einsum("bhqk,bkhd->bqhd", weights, vb, preferred_element_type=jnp.float32)
    return out.reshape(row_count, head_count, head_size)


def mix_request(projected, cache_rows, length, tap_table, window, head_size):
    row_count, feat_width = (projected.shape[0], projected.shape[2])
    time_order = (length + jnp.arange(window, dtype=jnp.int32)) % window
    earlier = cache_rows[:, time_order]
    key_rows = jnp.concatenate([earlier[0], projected[:, 1]], axis=0)
    value_rows = jnp.concatenate([earlier[1], projected[:, 2]], axis=0)
    head_count = feat_width // head_size
    attended = window_attend(
        projected[:, 0].reshape(row_count, head_count, head_size),
        key_rows.reshape(-1, head_count, head_size),
        value_rows.reshape(-1, head_count, head_size),
        length,
        window,
    ).reshape(row_count, feat_width)
    positions = jnp.arange(window + row_count, dtype=jnp.int32)
    alive_mask = (positions >= window - length)[:, None]
    masked_values = jnp.where(alive_mask, value_rows.astype(jnp.float32), jnp.float32(0.0))
    tap_count = tap_table.shape[0]
    convolved = jnp.zeros((row_count, feat_width), jnp.float32)
    for tap_index in range(tap_count):
        begin_row = window - (tap_count - 1) + tap_index
        convolved = (
            convolved + tap_table[tap_index] * masked_values[begin_row : begin_row + row_count]
        )
    mixed_heads = (attended + projected[:, 3].astype(jnp.float32) * convolved).astype(jnp.bfloat16)
    slot_source = (
        row_count - window + (jnp.arange(window, dtype=jnp.int32) - length - row_count) % window
    )
    renewed = jnp.stack([projected[:, 1], projected[:, 2]])[:, slot_source]
    return (mixed_heads, renewed)


def gather_packed(pieces):
    widths = [p.shape[1] for p in pieces]
    got = lax.all_gather(jnp.concatenate(pieces, axis=1), REQ, axis=0, tiled=True)
    parts = []
    start = 0
    for w in widths:
        parts.append(got[:, start : start + w])
        start += w
    return parts


def a2a_gather(x, axis):
    n = lax.axis_size(axis)
    return lax.all_to_all(jnp.tile(x[None], (n,) + (1,) * x.ndim), axis, 0, 0, tiled=True)


def req_gather_rows(x):
    by_z = a2a_gather(x, REQ[1])
    by_y = a2a_gather(by_z, REQ[0])
    return by_y.reshape((-1,) + x.shape[1:])


def tp_gather(x):
    nx = lax.axis_size("tpx")
    nc = lax.axis_size("tpc")
    by_chip = lax.all_to_all(jnp.tile(x[None], (nx, 1, 1)), "tpx", 0, 0, tiled=True)
    both = jnp.broadcast_to(by_chip[:, None], (nx, nc) + x.shape)
    got = lax.all_to_all(both, "tpc", 1, 1, tiled=True)
    return got.reshape((nx * nc * x.shape[0],) + x.shape[1:])


def tp_sum_scatter(x):
    nx = lax.axis_size("tpx")
    nc = lax.axis_size("tpc")
    rows = x.shape[0] // (nx * nc)
    parts = x.reshape((nx, nc, rows) + x.shape[1:])
    pair = lax.all_to_all(parts, "tpc", 1, 1, tiled=True)
    pair = pair.astype(jnp.float32).sum(axis=1).astype(jnp.bfloat16)
    chips = lax.all_to_all(pair, "tpx", 0, 0, tiled=True)
    return chips.astype(jnp.float32).sum(axis=0)


def local(
    tokens,
    norm_gain,
    ffn_gain,
    mix_weight,
    out_weight,
    ffn_weight,
    down_weight,
    conv_taps,
    past_cache,
    cached_len,
):
    feat_width = mix_weight.shape[2]
    ffn_width = ffn_weight.shape[2]
    rows = mix_weight.shape[0]
    mix_all = req_gather_rows(mix_weight.reshape(rows, -1))
    out_t, ffn_all, down_t = gather_packed(
        [out_weight.T, ffn_weight.reshape(rows, -1), down_weight.T]
    )
    normed_all = tp_gather(normed(tokens, norm_gain))
    row_total = normed_all.shape[0]
    projected = jnp.dot(normed_all, mix_all, preferred_element_type=jnp.float32)
    projected = projected.astype(jnp.bfloat16).reshape(row_total, 4, feat_width)
    mixed_heads, renewed = mix_request(projected, past_cache[0], cached_len[0], conv_taps, WIN, HD)
    attn_full = lax.dot_general(
        mixed_heads, out_t, (((1,), (1,)), ((), ())), preferred_element_type=jnp.float32
    )
    attn_part = tp_sum_scatter(attn_full.astype(jnp.bfloat16))
    residual = (tokens.astype(jnp.float32) + attn_part).astype(jnp.bfloat16)
    ffn_in = tp_gather(normed(residual, ffn_gain))
    gate_up = jnp.dot(ffn_in, ffn_all, preferred_element_type=jnp.float32)
    activated = (jax.nn.silu(gate_up[:, :ffn_width]) * gate_up[:, ffn_width:]).astype(jnp.bfloat16)
    ffn_full = lax.dot_general(
        activated, down_t, (((1,), (1,)), ((), ())), preferred_element_type=jnp.float32
    )
    ffn_part = tp_sum_scatter(ffn_full.astype(jnp.bfloat16))
    layer_out = (residual.astype(jnp.float32) + ffn_part).astype(jnp.bfloat16)
    return (layer_out, renewed[None])


def solution(mesh):
    n_req, n_tp = mesh.devices.shape
    ny = 4 if n_req % 4 == 0 else 1
    split = jax.sharding.Mesh(
        mesh.devices.reshape(ny, n_req // ny, n_tp // 2, 2), REQ + ("tpx", "tpc")
    )
    tp = ("tpx", "tpc")
    in_specs = (
        P(REQ + tp, None),
        P(),
        P(),
        P(REQ, None, tp),
        P(tp, REQ),
        P(REQ, None, tp),
        P(tp, REQ),
        P(None, tp),
        P(REQ, None, None, tp),
        P(REQ),
    )
    out_specs = (P(REQ + tp, None), P(REQ, None, None, tp))
    return jax.shard_map(local, mesh=split, in_specs=in_specs, out_specs=out_specs, check_vma=False)
```

```python
import math

import jax
import jax.numpy as jnp
from jax import lax
from jax.sharding import PartitionSpec as P

HD = 112
WIN = 64


def normed(row_vals, gain):
    floats = row_vals.astype(jnp.float32)
    scaled = floats * lax.rsqrt(jnp.mean(floats * floats, axis=-1, keepdims=True) + 1e-05)
    return (scaled * gain).astype(jnp.bfloat16)


def window_attend(queries, key_rows, value_rows, length, window):
    head_count, row_count, head_size = queries.shape
    nb = row_count // window
    score_scale = 1.0 / math.sqrt(head_size)
    qb = queries.reshape(head_count, nb, window, head_size)

    def blocks(rows):
        lo = rows[:, :row_count].reshape(head_count, nb, window, head_size)
        hi = rows[:, window:].reshape(head_count, nb, window, head_size)
        return jnp.concatenate([lo, hi], axis=2)

    kb = blocks(key_rows)
    vb = blocks(value_rows)
    scores = (
        jnp.einsum("hbqd,hbkd->hbqk", qb, kb, preferred_element_type=jnp.float32) * score_scale
    )
    i = jnp.arange(window, dtype=jnp.int32)[:, None]
    j = jnp.arange(2 * window, dtype=jnp.int32)[None, :]
    b = jnp.arange(nb, dtype=jnp.int32)[:, None, None]
    usable = (j > i)[None] & (j <= i + window)[None] & (b * window + j >= window - length)
    scores = jnp.where(usable[None], scores, -1e30)
    row_max = jnp.max(scores, axis=-1, keepdims=True)
    exponent = jnp.exp(scores - row_max)
    weights = (exponent / jnp.sum(exponent, axis=-1, keepdims=True)).astype(jnp.bfloat16)
    out = jnp.einsum("hbqk,hbkd->hbqd", weights, vb, preferred_element_type=jnp.float32)
    return out.reshape(head_count, row_count, head_size)


def mix_request(projected, cache_rows, length, tap_table, window, head_size):
    _, head_count, row_count, _ = projected.shape
    time_order = (length + jnp.arange(window, dtype=jnp.int32)) % window
    earlier = cache_rows[:, time_order].reshape(2, window, head_count, head_size)
    earlier = earlier.transpose(0, 2, 1, 3)
    key_rows = jnp.concatenate([earlier[0], projected[1]], axis=1)
    value_rows = jnp.concatenate([earlier[1], projected[2]], axis=1)
    attended = window_attend(projected[0], key_rows, value_rows, length, window)
    positions = jnp.arange(window + row_count, dtype=jnp.int32)
    alive_mask = (positions >= window - length)[None, :, None]
    masked_values = jnp.where(alive_mask, value_rows.astype(jnp.float32), jnp.float32(0.0))
    tap_count = tap_table.shape[0]
    taps = tap_table.reshape(tap_count, head_count, 1, head_size)
    convolved = jnp.zeros((head_count, row_count, head_size), jnp.float32)
    for tap_index in range(tap_count):
        begin_row = window - (tap_count - 1) + tap_index
        convolved = convolved + taps[tap_index] * masked_values[:, begin_row : begin_row + row_count]
    mixed_heads = (attended + projected[3].astype(jnp.float32) * convolved).astype(jnp.bfloat16)
    slot_source = (
        row_count - window + (jnp.arange(window, dtype=jnp.int32) - length - row_count) % window
    )
    renewed = projected[1:3][:, :, slot_source].transpose(0, 2, 1, 3)
    renewed = renewed.reshape(2, window, head_count * head_size)
    return (mixed_heads, renewed)


def gather_packed(pieces):
    widths = [p.shape[1] for p in pieces]
    got = lax.all_gather(jnp.concatenate(pieces, axis=1), "req", axis=0, tiled=True)
    parts = []
    start = 0
    for w in widths:
        parts.append(got[:, start : start + w])
        start += w
    return parts


def tp_gather(x):
    nx = lax.axis_size("tpx")
    nc = lax.axis_size("tpc")
    by_chip = lax.all_to_all(jnp.tile(x[None], (nx, 1, 1)), "tpx", 0, 0, tiled=True)
    both = jnp.broadcast_to(by_chip[:, None], (nx, nc) + x.shape)
    got = lax.all_to_all(both, "tpc", 1, 1, tiled=True)
    return got.reshape((nx * nc * x.shape[0],) + x.shape[1:])


def tp_sum_scatter(x):
    nx = lax.axis_size("tpx")
    nc = lax.axis_size("tpc")
    rows = x.shape[0] // (nx * nc)
    parts = x.reshape((nx, nc, rows) + x.shape[1:])
    pair = lax.all_to_all(parts, "tpc", 1, 1, tiled=True)
    pair = pair.astype(jnp.float32).sum(axis=1).astype(jnp.bfloat16)
    chips = lax.all_to_all(pair, "tpx", 0, 0, tiled=True)
    return chips.astype(jnp.float32).sum(axis=0)


def local(
    tokens,
    norm_gain,
    ffn_gain,
    mix_weight,
    out_weight,
    ffn_weight,
    down_weight,
    conv_taps,
    past_cache,
    cached_len,
):
    feat_width = mix_weight.shape[2]
    ffn_width = ffn_weight.shape[2]
    rows = mix_weight.shape[0]
    mix_all, out_t = gather_packed([mix_weight.reshape(rows, -1), out_weight.T])
    ffn_all, down_t = gather_packed([ffn_weight.reshape(rows, -1), down_weight.T])
    normed_all = tp_gather(normed(tokens, norm_gain))
    row_total = normed_all.shape[0]
    heads = feat_width // HD
    projected = jnp.einsum(
        "td,djhe->jhte",
        normed_all,
        mix_all.reshape(-1, 4, heads, HD),
        preferred_element_type=jnp.float32,
    ).astype(jnp.bfloat16)
    mixed_heads, renewed = mix_request(projected, past_cache[0], cached_len[0], conv_taps, WIN, HD)
    attn_full = jnp.einsum(
        "htd,fhd->tf",
        mixed_heads,
        out_t.reshape(out_t.shape[0], heads, HD),
        preferred_element_type=jnp.float32,
    )
    attn_part = tp_sum_scatter(attn_full.astype(jnp.bfloat16))
    residual = (tokens.astype(jnp.float32) + attn_part).astype(jnp.bfloat16)
    ffn_in = tp_gather(normed(residual, ffn_gain))
    gate_up = jnp.dot(ffn_in, ffn_all, preferred_element_type=jnp.float32)
    activated = (jax.nn.silu(gate_up[:, :ffn_width]) * gate_up[:, ffn_width:]).astype(jnp.bfloat16)
    ffn_full = lax.dot_general(
        activated, down_t, (((1,), (1,)), ((), ())), preferred_element_type=jnp.float32
    )
    ffn_part = tp_sum_scatter(ffn_full.astype(jnp.bfloat16))
    layer_out = (residual.astype(jnp.float32) + ffn_part).astype(jnp.bfloat16)
    return (layer_out, renewed[None])


def solution(mesh):
    n_req, n_tp = mesh.devices.shape
    split = jax.sharding.Mesh(mesh.devices.reshape(n_req, n_tp // 2, 2), ("req", "tpx", "tpc"))
    tp = ("tpx", "tpc")
    in_specs = (
        P(("req",) + tp, None),
        P(),
        P(),
        P("req", None, tp),
        P(tp, "req"),
        P("req", None, tp),
        P(tp, "req"),
        P(None, tp),
        P("req", None, None, tp),
        P("req"),
    )
    out_specs = (P(("req",) + tp, None), P("req", None, None, tp))
    return jax.shard_map(local, mesh=split, in_specs=in_specs, out_specs=out_specs, check_vma=False)
```

```python
import math

import jax
import jax.numpy as jnp
from jax import lax
from jax.sharding import PartitionSpec as P

HD = 112
WIN = 64


def normed(row_vals, gain):
    floats = row_vals.astype(jnp.float32)
    scaled = floats * lax.rsqrt(jnp.mean(floats * floats, axis=-1, keepdims=True) + 1e-05)
    return (scaled * gain).astype(jnp.bfloat16)


def window_attend(queries, key_rows, value_rows, length, window):
    row_count, head_count, head_size = queries.shape
    nb = row_count // window
    score_scale = 1.0 / math.sqrt(head_size)
    qb = queries.reshape(nb, window, head_count, head_size)

    def blocks(rows):
        lo = rows[:row_count].reshape(nb, window, head_count, head_size)
        hi = rows[window:].reshape(nb, window, head_count, head_size)
        return jnp.concatenate([lo, hi], axis=1)

    kb = blocks(key_rows)
    vb = blocks(value_rows)
    scores = (
        jnp.einsum("bqhd,bkhd->bhqk", qb, kb, preferred_element_type=jnp.float32) * score_scale
    )
    i = jnp.arange(window, dtype=jnp.int32)[:, None]
    j = jnp.arange(2 * window, dtype=jnp.int32)[None, :]
    b = jnp.arange(nb, dtype=jnp.int32)[:, None, None]
    usable = (j > i)[None] & (j <= i + window)[None] & (b * window + j >= window - length)
    scores = jnp.where(usable[:, None], scores, -1e30)
    row_max = jnp.max(scores, axis=-1, keepdims=True)
    exponent = jnp.exp(scores - row_max)
    weights = (exponent / jnp.sum(exponent, axis=-1, keepdims=True)).astype(jnp.bfloat16)
    out = jnp.einsum("bhqk,bkhd->bqhd", weights, vb, preferred_element_type=jnp.float32)
    return out.reshape(row_count, head_count, head_size)


def mix_request(projected, cache_rows, length, tap_table, window, head_size):
    row_count, feat_width = (projected.shape[0], projected.shape[2])
    time_order = (length + jnp.arange(window, dtype=jnp.int32)) % window
    earlier = cache_rows[:, time_order]
    key_rows = jnp.concatenate([earlier[0], projected[:, 1]], axis=0)
    value_rows = jnp.concatenate([earlier[1], projected[:, 2]], axis=0)
    head_count = feat_width // head_size
    attended = window_attend(
        projected[:, 0].reshape(row_count, head_count, head_size),
        key_rows.reshape(-1, head_count, head_size),
        value_rows.reshape(-1, head_count, head_size),
        length,
        window,
    ).reshape(row_count, feat_width)
    positions = jnp.arange(window + row_count, dtype=jnp.int32)
    alive_mask = (positions >= window - length)[:, None]
    masked_values = jnp.where(alive_mask, value_rows.astype(jnp.float32), jnp.float32(0.0))
    tap_count = tap_table.shape[0]
    convolved = jnp.zeros((row_count, feat_width), jnp.float32)
    for tap_index in range(tap_count):
        begin_row = window - (tap_count - 1) + tap_index
        convolved = (
            convolved + tap_table[tap_index] * masked_values[begin_row : begin_row + row_count]
        )
    mixed_heads = (attended + projected[:, 3].astype(jnp.float32) * convolved).astype(jnp.bfloat16)
    slot_source = (
        row_count - window + (jnp.arange(window, dtype=jnp.int32) - length - row_count) % window
    )
    renewed = jnp.stack([projected[:, 1], projected[:, 2]])[:, slot_source]
    return (mixed_heads, renewed)


def gather_packed(pieces):
    widths = [p.shape[1] for p in pieces]
    got = lax.all_gather(jnp.concatenate(pieces, axis=1), "req", axis=0, tiled=True)
    parts = []
    start = 0
    for w in widths:
        parts.append(got[:, start : start + w])
        start += w
    return parts


def ring_pass(x, axis, step):
    n = lax.axis_size(axis)
    return lax.ppermute(x, axis, [(i, (i + step) % n) for i in range(n)])


def x_gather(x):
    n = lax.axis_size("tpx")
    me = lax.axis_index("tpx")
    half = x.shape[-1] // 2
    from_left = ring_pass(x, "tpx", 1)
    from_right = ring_pass(x, "tpx", -1)
    far_a = ring_pass(from_left[..., :half], "tpx", 1)
    far_b = ring_pass(from_right[..., half:], "tpx", -1)
    far = jnp.concatenate([far_a, far_b], axis=-1)
    rel = jnp.stack([x, from_right, far, from_left])
    both = jnp.concatenate([rel, rel], axis=0)
    return lax.dynamic_slice_in_dim(both, (n - me) % n, n, axis=0)


def x_sum_scatter(parts):
    n = lax.axis_size("tpx")
    me = lax.axis_index("tpx")
    both = jnp.concatenate([parts, parts], axis=0)
    rel = lax.dynamic_slice_in_dim(both, me, n, axis=0)
    half = parts.shape[-1] // 2
    from_left = ring_pass(rel[1], "tpx", 1)
    from_right = ring_pass(rel[3], "tpx", -1)
    far_a = ring_pass(ring_pass(rel[2][..., :half], "tpx", 1), "tpx", 1)
    far_b = ring_pass(ring_pass(rel[2][..., half:], "tpx", -1), "tpx", -1)
    far = jnp.concatenate([far_a, far_b], axis=-1)
    f32 = jnp.float32
    return rel[0].astype(f32) + from_left.astype(f32) + from_right.astype(f32) + far.astype(f32)


def tp_gather(x):
    nx = lax.axis_size("tpx")
    nc = lax.axis_size("tpc")
    by_chip = x_gather(x)
    both = jnp.broadcast_to(by_chip[:, None], (nx, nc) + x.shape)
    got = lax.all_to_all(both, "tpc", 1, 1, tiled=True)
    return got.reshape((nx * nc * x.shape[0],) + x.shape[1:])


def tp_sum_scatter(x):
    nx = lax.axis_size("tpx")
    nc = lax.axis_size("tpc")
    rows = x.shape[0] // (nx * nc)
    parts = x.reshape((nx, nc, rows) + x.shape[1:])
    pair = lax.all_to_all(parts, "tpc", 1, 1, tiled=True)
    pair = pair.astype(jnp.float32).sum(axis=1).astype(jnp.bfloat16)
    return x_sum_scatter(pair)


def local(
    tokens,
    norm_gain,
    ffn_gain,
    mix_weight,
    out_weight,
    ffn_weight,
    down_weight,
    conv_taps,
    past_cache,
    cached_len,
):
    feat_width = mix_weight.shape[2]
    ffn_width = ffn_weight.shape[2]
    rows = mix_weight.shape[0]
    mix_all, out_t = gather_packed([mix_weight.reshape(rows, -1), out_weight.T])
    ffn_all, down_t = gather_packed([ffn_weight.reshape(rows, -1), down_weight.T])
    normed_all = tp_gather(normed(tokens, norm_gain))
    row_total = normed_all.shape[0]
    projected = jnp.dot(normed_all, mix_all, preferred_element_type=jnp.float32)
    projected = projected.astype(jnp.bfloat16).reshape(row_total, 4, feat_width)
    mixed_heads, renewed = mix_request(projected, past_cache[0], cached_len[0], conv_taps, WIN, HD)
    attn_full = lax.dot_general(
        mixed_heads, out_t, (((1,), (1,)), ((), ())), preferred_element_type=jnp.float32
    )
    attn_part = tp_sum_scatter(attn_full.astype(jnp.bfloat16))
    residual = (tokens.astype(jnp.float32) + attn_part).astype(jnp.bfloat16)
    ffn_in = tp_gather(normed(residual, ffn_gain))
    gate_up = jnp.dot(ffn_in, ffn_all, preferred_element_type=jnp.float32)
    activated = (jax.nn.silu(gate_up[:, :ffn_width]) * gate_up[:, ffn_width:]).astype(jnp.bfloat16)
    ffn_full = lax.dot_general(
        activated, down_t, (((1,), (1,)), ((), ())), preferred_element_type=jnp.float32
    )
    ffn_part = tp_sum_scatter(ffn_full.astype(jnp.bfloat16))
    layer_out = (residual.astype(jnp.float32) + ffn_part).astype(jnp.bfloat16)
    return (layer_out, renewed[None])


def solution(mesh):
    n_req, n_tp = mesh.devices.shape
    split = jax.sharding.Mesh(mesh.devices.reshape(n_req, n_tp // 2, 2), ("req", "tpx", "tpc"))
    tp = ("tpx", "tpc")
    in_specs = (
        P(("req",) + tp, None),
        P(),
        P(),
        P("req", None, tp),
        P(tp, "req"),
        P("req", None, tp),
        P(tp, "req"),
        P(None, tp),
        P("req", None, None, tp),
        P("req"),
    )
    out_specs = (P(("req",) + tp, None), P("req", None, None, tp))
    return jax.shard_map(local, mesh=split, in_specs=in_specs, out_specs=out_specs, check_vma=False)
```

```python
import math

import jax
import jax.numpy as jnp
from jax import lax
from jax.sharding import PartitionSpec as P

HD = 112
WIN = 64


def normed(row_vals, gain):
    floats = row_vals.astype(jnp.float32)
    scaled = floats * lax.rsqrt(jnp.mean(floats * floats, axis=-1, keepdims=True) + 1e-05)
    return (scaled * gain).astype(jnp.bfloat16)


def window_attend(queries, key_rows, value_rows, length, window):
    row_count, head_count, head_size = queries.shape
    nb = row_count // window
    score_scale = 1.0 / math.sqrt(head_size)
    qb = queries.reshape(nb, window, head_count, head_size)

    def blocks(rows):
        lo = rows[:row_count].reshape(nb, window, head_count, head_size)
        hi = rows[window:].reshape(nb, window, head_count, head_size)
        return jnp.concatenate([lo, hi], axis=1)

    kb = blocks(key_rows)
    vb = blocks(value_rows)
    scores = (
        jnp.einsum("bqhd,bkhd->bhqk", qb, kb, preferred_element_type=jnp.float32) * score_scale
    )
    i = jnp.arange(window, dtype=jnp.int32)[:, None]
    j = jnp.arange(2 * window, dtype=jnp.int32)[None, :]
    b = jnp.arange(nb, dtype=jnp.int32)[:, None, None]
    usable = (j > i)[None] & (j <= i + window)[None] & (b * window + j >= window - length)
    scores = jnp.where(usable[:, None], scores, -1e30)
    row_max = jnp.max(scores, axis=-1, keepdims=True)
    exponent = jnp.exp(scores - row_max)
    weights = (exponent / jnp.sum(exponent, axis=-1, keepdims=True)).astype(jnp.bfloat16)
    out = jnp.einsum("bhqk,bkhd->bqhd", weights, vb, preferred_element_type=jnp.float32)
    return out.reshape(row_count, head_count, head_size)


def mix_request(projected, cache_rows, length, tap_table, window, head_size):
    row_count, feat_width = (projected.shape[0], projected.shape[2])
    time_order = (length + jnp.arange(window, dtype=jnp.int32)) % window
    earlier = cache_rows[:, time_order]
    key_rows = jnp.concatenate([earlier[0], projected[:, 1]], axis=0)
    value_rows = jnp.concatenate([earlier[1], projected[:, 2]], axis=0)
    head_count = feat_width // head_size
    attended = window_attend(
        projected[:, 0].reshape(row_count, head_count, head_size),
        key_rows.reshape(-1, head_count, head_size),
        value_rows.reshape(-1, head_count, head_size),
        length,
        window,
    ).reshape(row_count, feat_width)
    positions = jnp.arange(window + row_count, dtype=jnp.int32)
    alive_mask = (positions >= window - length)[:, None]
    masked_values = jnp.where(alive_mask, value_rows.astype(jnp.float32), jnp.float32(0.0))
    tap_count = tap_table.shape[0]
    convolved = jnp.zeros((row_count, feat_width), jnp.float32)
    for tap_index in range(tap_count):
        begin_row = window - (tap_count - 1) + tap_index
        convolved = (
            convolved + tap_table[tap_index] * masked_values[begin_row : begin_row + row_count]
        )
    mixed_heads = (attended + projected[:, 3].astype(jnp.float32) * convolved).astype(jnp.bfloat16)
    slot_source = (
        row_count - window + (jnp.arange(window, dtype=jnp.int32) - length - row_count) % window
    )
    renewed = jnp.stack([projected[:, 1], projected[:, 2]])[:, slot_source]
    return (mixed_heads, renewed)


def gather_packed(pieces):
    widths = [p.shape[1] for p in pieces]
    got = lax.all_gather(jnp.concatenate(pieces, axis=1), "req", axis=0, tiled=True)
    parts = []
    start = 0
    for w in widths:
        parts.append(got[:, start : start + w])
        start += w
    return parts


def tp_gather(x):
    nx = lax.axis_size("tpx")
    nc = lax.axis_size("tpc")
    by_chip = lax.all_to_all(jnp.tile(x[None], (nx, 1, 1)), "tpx", 0, 0, tiled=True)
    both = jnp.broadcast_to(by_chip[:, None], (nx, nc) + x.shape)
    got = lax.all_to_all(both, "tpc", 1, 1, tiled=True)
    return got.reshape((nx * nc * x.shape[0],) + x.shape[1:])


def tp_sum_scatter(x):
    nx = lax.axis_size("tpx")
    nc = lax.axis_size("tpc")
    rows = x.shape[0] // (nx * nc)
    parts = x.reshape((nx, nc, rows) + x.shape[1:])
    pair = lax.all_to_all(parts, "tpc", 1, 1, tiled=True)
    pair = pair.astype(jnp.float32).sum(axis=1).astype(jnp.bfloat16)
    chips = lax.all_to_all(pair, "tpx", 0, 0, tiled=True)
    return chips.astype(jnp.float32).sum(axis=0)


def core_swap(x):
    return lax.ppermute(x, "tpc", [(0, 1), (1, 0)])


def mlp_rows(rows, ffn_all, down_t, ffn_width):
    gate_up = jnp.dot(rows, ffn_all, preferred_element_type=jnp.float32)
    activated = (jax.nn.silu(gate_up[:, :ffn_width]) * gate_up[:, ffn_width:]).astype(jnp.bfloat16)
    out = lax.dot_general(
        activated, down_t, (((1,), (1,)), ((), ())), preferred_element_type=jnp.float32
    )
    return out.astype(jnp.bfloat16)


def local(
    tokens,
    norm_gain,
    ffn_gain,
    mix_weight,
    out_weight,
    ffn_weight,
    down_weight,
    conv_taps,
    past_cache,
    cached_len,
):
    feat_width = mix_weight.shape[2]
    ffn_width = ffn_weight.shape[2]
    rows = mix_weight.shape[0]
    mix_all, out_t = gather_packed([mix_weight.reshape(rows, -1), out_weight.T])
    ffn_all, down_t = gather_packed([ffn_weight.reshape(rows, -1), down_weight.T])
    normed_all = tp_gather(normed(tokens, norm_gain))
    row_total = normed_all.shape[0]
    projected = jnp.dot(normed_all, mix_all, preferred_element_type=jnp.float32)
    projected = projected.astype(jnp.bfloat16).reshape(row_total, 4, feat_width)
    mixed_heads, renewed = mix_request(projected, past_cache[0], cached_len[0], conv_taps, WIN, HD)
    attn_full = lax.dot_general(
        mixed_heads, out_t, (((1,), (1,)), ((), ())), preferred_element_type=jnp.float32
    )
    attn_part = tp_sum_scatter(attn_full.astype(jnp.bfloat16))
    residual = (tokens.astype(jnp.float32) + attn_part).astype(jnp.bfloat16)
    nx = lax.axis_size("tpx")
    mine = lax.all_to_all(
        jnp.tile(normed(residual, ffn_gain)[None], (nx, 1, 1)), "tpx", 0, 0, tiled=True
    )
    flat = mine.reshape((-1,) + mine.shape[2:])
    theirs = core_swap(flat)
    part_mine = mlp_rows(flat, ffn_all, down_t, ffn_width)
    part_theirs = mlp_rows(theirs, ffn_all, down_t, ffn_width)
    back = core_swap(part_theirs)
    pair = (part_mine.astype(jnp.float32) + back.astype(jnp.float32)).astype(jnp.bfloat16)
    chips = lax.all_to_all(pair.reshape(mine.shape), "tpx", 0, 0, tiled=True)
    ffn_part = chips.astype(jnp.float32).sum(axis=0)
    layer_out = (residual.astype(jnp.float32) + ffn_part).astype(jnp.bfloat16)
    return (layer_out, renewed[None])


def solution(mesh):
    n_req, n_tp = mesh.devices.shape
    split = jax.sharding.Mesh(mesh.devices.reshape(n_req, n_tp // 2, 2), ("req", "tpx", "tpc"))
    tp = ("tpx", "tpc")
    in_specs = (
        P(("req",) + tp, None),
        P(),
        P(),
        P("req", None, tp),
        P(tp, "req"),
        P("req", None, tp),
        P(tp, "req"),
        P(None, tp),
        P("req", None, None, tp),
        P("req"),
    )
    out_specs = (P(("req",) + tp, None), P("req", None, None, tp))
    return jax.shard_map(local, mesh=split, in_specs=in_specs, out_specs=out_specs, check_vma=False)
```

```python
import math

import jax
import jax.numpy as jnp
from jax import lax
from jax.sharding import PartitionSpec as P

HD = 112
WIN = 64
REQ = ("ry", "rz")


def normed(row_vals, gain):
    floats = row_vals.astype(jnp.float32)
    scaled = floats * lax.rsqrt(jnp.mean(floats * floats, axis=-1, keepdims=True) + 1e-05)
    return (scaled * gain).astype(jnp.bfloat16)


def window_attend(queries, key_rows, value_rows, length, window):
    row_count, head_count, head_size = queries.shape
    nb = row_count // window
    score_scale = 1.0 / math.sqrt(head_size)
    qb = queries.reshape(nb, window, head_count, head_size)

    def blocks(rows):
        lo = rows[:row_count].reshape(nb, window, head_count, head_size)
        hi = rows[window:].reshape(nb, window, head_count, head_size)
        return jnp.concatenate([lo, hi], axis=1)

    kb = blocks(key_rows)
    vb = blocks(value_rows)
    scores = (
        jnp.einsum("bqhd,bkhd->bhqk", qb, kb, preferred_element_type=jnp.float32) * score_scale
    )
    i = jnp.arange(window, dtype=jnp.int32)[:, None]
    j = jnp.arange(2 * window, dtype=jnp.int32)[None, :]
    b = jnp.arange(nb, dtype=jnp.int32)[:, None, None]
    usable = (j > i)[None] & (j <= i + window)[None] & (b * window + j >= window - length)
    scores = jnp.where(usable[:, None], scores, -1e30)
    row_max = jnp.max(scores, axis=-1, keepdims=True)
    exponent = jnp.exp(scores - row_max)
    weights = (exponent / jnp.sum(exponent, axis=-1, keepdims=True)).astype(jnp.bfloat16)
    out = jnp.einsum("bhqk,bkhd->bqhd", weights, vb, preferred_element_type=jnp.float32)
    return out.reshape(row_count, head_count, head_size)


def mix_request(projected, cache_rows, length, tap_table, window, head_size):
    row_count, feat_width = (projected.shape[0], projected.shape[2])
    time_order = (length + jnp.arange(window, dtype=jnp.int32)) % window
    earlier = cache_rows[:, time_order]
    key_rows = jnp.concatenate([earlier[0], projected[:, 1]], axis=0)
    value_rows = jnp.concatenate([earlier[1], projected[:, 2]], axis=0)
    head_count = feat_width // head_size
    attended = window_attend(
        projected[:, 0].reshape(row_count, head_count, head_size),
        key_rows.reshape(-1, head_count, head_size),
        value_rows.reshape(-1, head_count, head_size),
        length,
        window,
    ).reshape(row_count, feat_width)
    positions = jnp.arange(window + row_count, dtype=jnp.int32)
    alive_mask = (positions >= window - length)[:, None]
    masked_values = jnp.where(alive_mask, value_rows.astype(jnp.float32), jnp.float32(0.0))
    tap_count = tap_table.shape[0]
    convolved = jnp.zeros((row_count, feat_width), jnp.float32)
    for tap_index in range(tap_count):
        begin_row = window - (tap_count - 1) + tap_index
        convolved = (
            convolved + tap_table[tap_index] * masked_values[begin_row : begin_row + row_count]
        )
    mixed_heads = (attended + projected[:, 3].astype(jnp.float32) * convolved).astype(jnp.bfloat16)
    slot_source = (
        row_count - window + (jnp.arange(window, dtype=jnp.int32) - length - row_count) % window
    )
    renewed = jnp.stack([projected[:, 1], projected[:, 2]])[:, slot_source]
    return (mixed_heads, renewed)


def gather_packed(pieces):
    widths = [p.shape[1] for p in pieces]
    by_z = lax.all_gather(jnp.concatenate(pieces, axis=1), REQ[1], axis=0, tiled=True)
    got = lax.all_gather(by_z, REQ[0], axis=0, tiled=True)
    parts = []
    start = 0
    for w in widths:
        parts.append(got[:, start : start + w])
        start += w
    return parts


def tp_gather(x):
    nx = lax.axis_size("tpx")
    nc = lax.axis_size("tpc")
    by_chip = lax.all_to_all(jnp.tile(x[None], (nx, 1, 1)), "tpx", 0, 0, tiled=True)
    both = jnp.broadcast_to(by_chip[:, None], (nx, nc) + x.shape)
    got = lax.all_to_all(both, "tpc", 1, 1, tiled=True)
    return got.reshape((nx * nc * x.shape[0],) + x.shape[1:])


def tp_sum_scatter(x):
    nx = lax.axis_size("tpx")
    nc = lax.axis_size("tpc")
    rows = x.shape[0] // (nx * nc)
    parts = x.reshape((nx, nc, rows) + x.shape[1:])
    pair = lax.all_to_all(parts, "tpc", 1, 1, tiled=True)
    pair = pair.astype(jnp.float32).sum(axis=1).astype(jnp.bfloat16)
    chips = lax.all_to_all(pair, "tpx", 0, 0, tiled=True)
    return chips.astype(jnp.float32).sum(axis=0)


def core_swap(x):
    return lax.ppermute(x, "tpc", [(0, 1), (1, 0)])


def mlp_rows(rows, ffn_all, down_t, ffn_width):
    gate_up = jnp.dot(rows, ffn_all, preferred_element_type=jnp.float32)
    activated = (jax.nn.silu(gate_up[:, :ffn_width]) * gate_up[:, ffn_width:]).astype(jnp.bfloat16)
    out = lax.dot_general(
        activated, down_t, (((1,), (1,)), ((), ())), preferred_element_type=jnp.float32
    )
    return out.astype(jnp.bfloat16)


def local(
    tokens,
    norm_gain,
    ffn_gain,
    mix_weight,
    out_weight,
    ffn_weight,
    down_weight,
    conv_taps,
    past_cache,
    cached_len,
):
    feat_width = mix_weight.shape[2]
    ffn_width = ffn_weight.shape[2]
    rows = mix_weight.shape[0]
    mix_all, out_t = gather_packed([mix_weight.reshape(rows, -1), out_weight.T])
    ffn_all, down_t = gather_packed([ffn_weight.reshape(rows, -1), down_weight.T])
    normed_all = tp_gather(normed(tokens, norm_gain))
    row_total = normed_all.shape[0]
    projected = jnp.dot(normed_all, mix_all, preferred_element_type=jnp.float32)
    projected = projected.astype(jnp.bfloat16).reshape(row_total, 4, feat_width)
    mixed_heads, renewed = mix_request(projected, past_cache[0], cached_len[0], conv_taps, WIN, HD)
    attn_full = lax.dot_general(
        mixed_heads, out_t, (((1,), (1,)), ((), ())), preferred_element_type=jnp.float32
    )
    attn_part = tp_sum_scatter(attn_full.astype(jnp.bfloat16))
    residual = (tokens.astype(jnp.float32) + attn_part).astype(jnp.bfloat16)
    nx = lax.axis_size("tpx")
    mine = lax.all_to_all(
        jnp.tile(normed(residual, ffn_gain)[None], (nx, 1, 1)), "tpx", 0, 0, tiled=True
    )
    flat = mine.reshape((-1,) + mine.shape[2:])
    theirs = core_swap(flat)
    part_mine = mlp_rows(flat, ffn_all, down_t, ffn_width)
    part_theirs = mlp_rows(theirs, ffn_all, down_t, ffn_width)
    back = core_swap(part_theirs)
    pair = (part_mine.astype(jnp.float32) + back.astype(jnp.float32)).astype(jnp.bfloat16)
    chips = lax.all_to_all(pair.reshape(mine.shape), "tpx", 0, 0, tiled=True)
    ffn_part = chips.astype(jnp.float32).sum(axis=0)
    layer_out = (residual.astype(jnp.float32) + ffn_part).astype(jnp.bfloat16)
    return (layer_out, renewed[None])


def solution(mesh):
    n_req, n_tp = mesh.devices.shape
    ny = 4 if n_req % 4 == 0 else 1
    split = jax.sharding.Mesh(
        mesh.devices.reshape(ny, n_req // ny, n_tp // 2, 2), REQ + ("tpx", "tpc")
    )
    tp = ("tpx", "tpc")
    in_specs = (
        P(REQ + tp, None),
        P(),
        P(),
        P(REQ, None, tp),
        P(tp, REQ),
        P(REQ, None, tp),
        P(tp, REQ),
        P(None, tp),
        P(REQ, None, None, tp),
        P(REQ),
    )
    out_specs = (P(REQ + tp, None), P(REQ, None, None, tp))
    return jax.shard_map(local, mesh=split, in_specs=in_specs, out_specs=out_specs, check_vma=False)
```

```python
import math

import jax
import jax.numpy as jnp
from jax import lax
from jax.sharding import PartitionSpec as P

HD = 112
WIN = 64


def normed(row_vals, gain):
    floats = row_vals.astype(jnp.float32)
    scaled = floats * lax.rsqrt(jnp.mean(floats * floats, axis=-1, keepdims=True) + 1e-05)
    return (scaled * gain).astype(jnp.bfloat16)


def window_attend(queries, key_rows, value_rows, length, window):
    row_count, head_count, head_size = queries.shape
    nb = row_count // window
    score_scale = 1.0 / math.sqrt(head_size)
    qb = queries.reshape(nb, window, head_count, head_size)

    def blocks(rows):
        lo = rows[:row_count].reshape(nb, window, head_count, head_size)
        hi = rows[window:].reshape(nb, window, head_count, head_size)
        return jnp.concatenate([lo, hi], axis=1)

    kb = blocks(key_rows)
    vb = blocks(value_rows)
    scores = (
        jnp.einsum("bqhd,bkhd->bhqk", qb, kb, preferred_element_type=jnp.float32) * score_scale
    )
    i = jnp.arange(window, dtype=jnp.int32)[:, None]
    j = jnp.arange(2 * window, dtype=jnp.int32)[None, :]
    b = jnp.arange(nb, dtype=jnp.int32)[:, None, None]
    usable = (j > i)[None] & (j <= i + window)[None] & (b * window + j >= window - length)
    scores = jnp.where(usable[:, None], scores, -1e30)
    row_max = jnp.max(scores, axis=-1, keepdims=True)
    exponent = jnp.exp(scores - row_max)
    weights = (exponent / jnp.sum(exponent, axis=-1, keepdims=True)).astype(jnp.bfloat16)
    out = jnp.einsum("bhqk,bkhd->bqhd", weights, vb, preferred_element_type=jnp.float32)
    return out.reshape(row_count, head_count, head_size)


def mix_request(projected, cache_rows, length, tap_table, window, head_size):
    row_count, feat_width = (projected.shape[0], projected.shape[2])
    time_order = (length + jnp.arange(window, dtype=jnp.int32)) % window
    earlier = cache_rows[:, time_order]
    key_rows = jnp.concatenate([earlier[0], projected[:, 1]], axis=0)
    value_rows = jnp.concatenate([earlier[1], projected[:, 2]], axis=0)
    head_count = feat_width // head_size
    attended = window_attend(
        projected[:, 0].reshape(row_count, head_count, head_size),
        key_rows.reshape(-1, head_count, head_size),
        value_rows.reshape(-1, head_count, head_size),
        length,
        window,
    ).reshape(row_count, feat_width)
    positions = jnp.arange(window + row_count, dtype=jnp.int32)
    alive_mask = (positions >= window - length)[:, None]
    masked_values = jnp.where(alive_mask, value_rows.astype(jnp.float32), jnp.float32(0.0))
    tap_count = tap_table.shape[0]
    convolved = jnp.zeros((row_count, feat_width), jnp.float32)
    for tap_index in range(tap_count):
        begin_row = window - (tap_count - 1) + tap_index
        convolved = (
            convolved + tap_table[tap_index] * masked_values[begin_row : begin_row + row_count]
        )
    mixed_heads = (attended + projected[:, 3].astype(jnp.float32) * convolved).astype(jnp.bfloat16)
    slot_source = (
        row_count - window + (jnp.arange(window, dtype=jnp.int32) - length - row_count) % window
    )
    renewed = jnp.stack([projected[:, 1], projected[:, 2]])[:, slot_source]
    return (mixed_heads, renewed)


def gather_packed(pieces):
    widths = [p.shape[1] for p in pieces]
    got = lax.all_gather(jnp.concatenate(pieces, axis=1), "req", axis=0, tiled=True)
    parts = []
    start = 0
    for w in widths:
        parts.append(got[:, start : start + w])
        start += w
    return parts


def tp_gather(x):
    nx = lax.axis_size("tpx")
    nc = lax.axis_size("tpc")
    by_chip = lax.all_to_all(jnp.tile(x[None], (nx, 1, 1)), "tpx", 0, 0, tiled=True)
    both = jnp.broadcast_to(by_chip[:, None], (nx, nc) + x.shape)
    got = lax.all_to_all(both, "tpc", 1, 1, tiled=True)
    return got.reshape((nx * nc * x.shape[0],) + x.shape[1:])


def tp_sum_scatter(x):
    nx = lax.axis_size("tpx")
    nc = lax.axis_size("tpc")
    rows = x.shape[0] // (nx * nc)
    parts = x.reshape((nx, nc, rows) + x.shape[1:])
    pair = lax.all_to_all(parts, "tpc", 1, 1, tiled=True)
    pair = pair.astype(jnp.float32).sum(axis=1).astype(jnp.bfloat16)
    chips = lax.all_to_all(pair, "tpx", 0, 0, tiled=True)
    return chips.astype(jnp.float32).sum(axis=0)


def core_swap(x):
    return lax.ppermute(x, "tpc", [(0, 1), (1, 0)])


def mlp_rows(rows, ffn_all, down_t, ffn_width):
    gate_up = jnp.dot(rows, ffn_all, preferred_element_type=jnp.float32)
    activated = (jax.nn.silu(gate_up[:, :ffn_width]) * gate_up[:, ffn_width:]).astype(jnp.bfloat16)
    out = lax.dot_general(
        activated, down_t, (((1,), (1,)), ((), ())), preferred_element_type=jnp.float32
    )
    return out.astype(jnp.bfloat16)


def local(
    tokens,
    norm_gain,
    ffn_gain,
    mix_weight,
    out_weight,
    ffn_weight,
    down_weight,
    conv_taps,
    past_cache,
    cached_len,
):
    feat_width = mix_weight.shape[2]
    ffn_width = ffn_weight.shape[2]
    rows = mix_weight.shape[0]
    mix_all, out_t = gather_packed([mix_weight.reshape(rows, -1), out_weight.T])
    ffn_all, down_t = gather_packed([ffn_weight.reshape(rows, -1), down_weight.T])
    normed_all = tp_gather(normed(tokens, norm_gain))
    row_total = normed_all.shape[0]
    projected = jnp.dot(normed_all, mix_all, preferred_element_type=jnp.float32)
    projected = projected.astype(jnp.bfloat16).reshape(row_total, 4, feat_width)
    mixed_heads, renewed = mix_request(projected, past_cache[0], cached_len[0], conv_taps, WIN, HD)
    attn_full = lax.dot_general(
        mixed_heads, out_t, (((1,), (1,)), ((), ())), preferred_element_type=jnp.float32
    )
    attn_part = tp_sum_scatter(attn_full.astype(jnp.bfloat16))
    residual = (tokens.astype(jnp.float32) + attn_part).astype(jnp.bfloat16)
    nx = lax.axis_size("tpx")
    mine = lax.all_to_all(
        jnp.tile(normed(residual, ffn_gain)[None], (nx, 1, 1)), "tpx", 0, 0, tiled=True
    )
    flat = mine.reshape((-1,) + mine.shape[2:])
    theirs = core_swap(flat)
    part_mine = mlp_rows(flat, ffn_all, down_t, ffn_width)
    part_theirs = mlp_rows(theirs, ffn_all, down_t, ffn_width)
    back = core_swap(part_theirs)
    pair = (part_mine.astype(jnp.float32) + back.astype(jnp.float32)).astype(jnp.bfloat16)
    ffn_part = lax.psum_scatter(pair, "tpx", scatter_dimension=0, tiled=True).astype(jnp.float32)
    layer_out = (residual.astype(jnp.float32) + ffn_part).astype(jnp.bfloat16)
    return (layer_out, renewed[None])


def solution(mesh):
    n_req, n_tp = mesh.devices.shape
    split = jax.sharding.Mesh(mesh.devices.reshape(n_req, n_tp // 2, 2), ("req", "tpx", "tpc"))
    tp = ("tpx", "tpc")
    in_specs = (
        P(("req",) + tp, None),
        P(),
        P(),
        P("req", None, tp),
        P(tp, "req"),
        P("req", None, tp),
        P(tp, "req"),
        P(None, tp),
        P("req", None, None, tp),
        P("req"),
    )
    out_specs = (P(("req",) + tp, None), P("req", None, None, tp))
    return jax.shard_map(local, mesh=split, in_specs=in_specs, out_specs=out_specs, check_vma=False)
```

```python
import math

import jax
import jax.numpy as jnp
from jax import lax
from jax.sharding import PartitionSpec as P

HD = 112
WIN = 64


def normed(row_vals, gain):
    floats = row_vals.astype(jnp.float32)
    scaled = floats * lax.rsqrt(jnp.mean(floats * floats, axis=-1, keepdims=True) + 1e-05)
    return (scaled * gain).astype(jnp.bfloat16)


def window_attend(queries, key_rows, value_rows, length, window):
    row_count, head_count, head_size = queries.shape
    nb = row_count // window
    score_scale = 1.0 / math.sqrt(head_size)
    qb = queries.reshape(nb, window, head_count, head_size)

    def blocks(rows):
        lo = rows[:row_count].reshape(nb, window, head_count, head_size)
        hi = rows[window:].reshape(nb, window, head_count, head_size)
        return jnp.concatenate([lo, hi], axis=1)

    kb = blocks(key_rows)
    vb = blocks(value_rows)
    scores = (
        jnp.einsum("bqhd,bkhd->bhqk", qb, kb, preferred_element_type=jnp.float32) * score_scale
    )
    i = jnp.arange(window, dtype=jnp.int32)[:, None]
    j = jnp.arange(2 * window, dtype=jnp.int32)[None, :]
    b = jnp.arange(nb, dtype=jnp.int32)[:, None, None]
    usable = (j > i)[None] & (j <= i + window)[None] & (b * window + j >= window - length)
    scores = jnp.where(usable[:, None], scores, -1e30)
    row_max = jnp.max(scores, axis=-1, keepdims=True)
    exponent = jnp.exp(scores - row_max)
    weights = (exponent / jnp.sum(exponent, axis=-1, keepdims=True)).astype(jnp.bfloat16)
    out = jnp.einsum("bhqk,bkhd->bqhd", weights, vb, preferred_element_type=jnp.float32)
    return out.reshape(row_count, head_count, head_size)


def mix_request(projected, cache_rows, length, tap_table, window, head_size):
    row_count, feat_width = (projected.shape[0], projected.shape[2])
    time_order = (length + jnp.arange(window, dtype=jnp.int32)) % window
    earlier = cache_rows[:, time_order]
    key_rows = jnp.concatenate([earlier[0], projected[:, 1]], axis=0)
    value_rows = jnp.concatenate([earlier[1], projected[:, 2]], axis=0)
    head_count = feat_width // head_size
    attended = window_attend(
        projected[:, 0].reshape(row_count, head_count, head_size),
        key_rows.reshape(-1, head_count, head_size),
        value_rows.reshape(-1, head_count, head_size),
        length,
        window,
    ).reshape(row_count, feat_width)
    positions = jnp.arange(window + row_count, dtype=jnp.int32)
    alive_mask = (positions >= window - length)[:, None]
    masked_values = jnp.where(alive_mask, value_rows.astype(jnp.float32), jnp.float32(0.0))
    tap_count = tap_table.shape[0]
    convolved = jnp.zeros((row_count, feat_width), jnp.float32)
    for tap_index in range(tap_count):
        begin_row = window - (tap_count - 1) + tap_index
        convolved = (
            convolved + tap_table[tap_index] * masked_values[begin_row : begin_row + row_count]
        )
    mixed_heads = (attended + projected[:, 3].astype(jnp.float32) * convolved).astype(jnp.bfloat16)
    slot_source = (
        row_count - window + (jnp.arange(window, dtype=jnp.int32) - length - row_count) % window
    )
    renewed = jnp.stack([projected[:, 1], projected[:, 2]])[:, slot_source]
    return (mixed_heads, renewed)


def gather_packed(pieces):
    widths = [p.shape[1] for p in pieces]
    got = lax.all_gather(jnp.concatenate(pieces, axis=1), "req", axis=0, tiled=True)
    parts = []
    start = 0
    for w in widths:
        parts.append(got[:, start : start + w])
        start += w
    return parts


def tp_gather(x):
    nx = lax.axis_size("tpx")
    nc = lax.axis_size("tpc")
    by_chip = lax.all_to_all(jnp.tile(x[None], (nx, 1, 1)), "tpx", 0, 0, tiled=True)
    both = jnp.broadcast_to(by_chip[:, None], (nx, nc) + x.shape)
    got = lax.all_to_all(both, "tpc", 1, 1, tiled=True)
    return got.reshape((nx * nc * x.shape[0],) + x.shape[1:])


def tp_sum_scatter(x):
    nx = lax.axis_size("tpx")
    nc = lax.axis_size("tpc")
    rows = x.shape[0] // (nx * nc)
    parts = x.reshape((nx, nc, rows) + x.shape[1:])
    pair = lax.all_to_all(parts, "tpc", 1, 1, tiled=True)
    pair = pair.astype(jnp.float32).sum(axis=1).astype(jnp.bfloat16)
    chips = lax.all_to_all(pair, "tpx", 0, 0, tiled=True)
    return chips.astype(jnp.float32).sum(axis=0)


def core_swap(x):
    return lax.ppermute(x, "tpc", [(0, 1), (1, 0)])


def mlp_rows(rows, ffn_all, down_t, ffn_width):
    gate_up = jnp.dot(rows, ffn_all, preferred_element_type=jnp.float32)
    activated = (jax.nn.silu(gate_up[:, :ffn_width]) * gate_up[:, ffn_width:]).astype(jnp.bfloat16)
    out = lax.dot_general(
        activated, down_t, (((1,), (1,)), ((), ())), preferred_element_type=jnp.float32
    )
    return out.astype(jnp.bfloat16)


def local(
    tokens,
    norm_gain,
    ffn_gain,
    mix_weight,
    out_weight,
    ffn_weight,
    down_weight,
    conv_taps,
    past_cache,
    cached_len,
):
    feat_width = mix_weight.shape[2]
    ffn_width = ffn_weight.shape[2]
    rows = mix_weight.shape[0]
    mix_all, out_t = gather_packed([mix_weight.reshape(rows, -1), out_weight.T])
    ffn_all, down_t = gather_packed([ffn_weight.reshape(rows, -1), down_weight.T])
    normed_all = tp_gather(normed(tokens, norm_gain))
    row_total = normed_all.shape[0]
    projected = jnp.dot(normed_all, mix_all, preferred_element_type=jnp.float32)
    projected = projected.astype(jnp.bfloat16).reshape(row_total, 4, feat_width)
    mixed_heads, renewed = mix_request(projected, past_cache[0], cached_len[0], conv_taps, WIN, HD)
    nx = lax.axis_size("tpx")
    nc = lax.axis_size("tpc")
    me_c = lax.axis_index("tpc")
    by_core = mixed_heads.reshape(nx, nc, -1, feat_width)
    mine_rows = lax.dynamic_index_in_dim(by_core, me_c, axis=1, keepdims=False)
    their_rows = lax.dynamic_index_in_dim(by_core, 1 - me_c, axis=1, keepdims=False)

    def out_rows(r):
        return lax.dot_general(
            r.reshape(-1, feat_width), out_t, (((1,), (1,)), ((), ())),
            preferred_element_type=jnp.float32,
        ).astype(jnp.bfloat16)

    back = core_swap(out_rows(their_rows))
    pair = (out_rows(mine_rows).astype(jnp.float32) + back.astype(jnp.float32)).astype(jnp.bfloat16)
    chips = lax.all_to_all(pair.reshape((nx, -1) + pair.shape[1:]), "tpx", 0, 0, tiled=True)
    attn_part = chips.astype(jnp.float32).sum(axis=0)
    residual = (tokens.astype(jnp.float32) + attn_part).astype(jnp.bfloat16)
    nx = lax.axis_size("tpx")
    mine = lax.all_to_all(
        jnp.tile(normed(residual, ffn_gain)[None], (nx, 1, 1)), "tpx", 0, 0, tiled=True
    )
    flat = mine.reshape((-1,) + mine.shape[2:])
    theirs = core_swap(flat)
    part_mine = mlp_rows(flat, ffn_all, down_t, ffn_width)
    part_theirs = mlp_rows(theirs, ffn_all, down_t, ffn_width)
    back = core_swap(part_theirs)
    pair = (part_mine.astype(jnp.float32) + back.astype(jnp.float32)).astype(jnp.bfloat16)
    ffn_part = lax.psum_scatter(pair, "tpx", scatter_dimension=0, tiled=True).astype(jnp.float32)
    layer_out = (residual.astype(jnp.float32) + ffn_part).astype(jnp.bfloat16)
    return (layer_out, renewed[None])


def solution(mesh):
    n_req, n_tp = mesh.devices.shape
    split = jax.sharding.Mesh(mesh.devices.reshape(n_req, n_tp // 2, 2), ("req", "tpx", "tpc"))
    tp = ("tpx", "tpc")
    in_specs = (
        P(("req",) + tp, None),
        P(),
        P(),
        P("req", None, tp),
        P(tp, "req"),
        P("req", None, tp),
        P(tp, "req"),
        P(None, tp),
        P("req", None, None, tp),
        P("req"),
    )
    out_specs = (P(("req",) + tp, None), P("req", None, None, tp))
    return jax.shard_map(local, mesh=split, in_specs=in_specs, out_specs=out_specs, check_vma=False)
```

```python
import math

import jax
import jax.numpy as jnp
from jax import lax
from jax.sharding import PartitionSpec as P

HD = 112
WIN = 64


def normed(row_vals, gain):
    floats = row_vals.astype(jnp.float32)
    scaled = floats * lax.rsqrt(jnp.mean(floats * floats, axis=-1, keepdims=True) + 1e-05)
    return (scaled * gain).astype(jnp.bfloat16)


def window_attend(queries, key_rows, value_rows, length, window):
    row_count, head_count, head_size = queries.shape
    nb = row_count // window
    score_scale = 1.0 / math.sqrt(head_size)
    qb = queries.reshape(nb, window, head_count, head_size)

    def blocks(rows):
        lo = rows[:row_count].reshape(nb, window, head_count, head_size)
        hi = rows[window:].reshape(nb, window, head_count, head_size)
        return jnp.concatenate([lo, hi], axis=1)

    kb = blocks(key_rows)
    vb = blocks(value_rows)
    scores = (
        jnp.einsum("bqhd,bkhd->bhqk", qb, kb, preferred_element_type=jnp.float32) * score_scale
    )
    i = jnp.arange(window, dtype=jnp.int32)[:, None]
    j = jnp.arange(2 * window, dtype=jnp.int32)[None, :]
    b = jnp.arange(nb, dtype=jnp.int32)[:, None, None]
    usable = (j > i)[None] & (j <= i + window)[None] & (b * window + j >= window - length)
    scores = jnp.where(usable[:, None], scores, -1e30)
    row_max = jnp.max(scores, axis=-1, keepdims=True)
    exponent = jnp.exp(scores - row_max)
    weights = (exponent / jnp.sum(exponent, axis=-1, keepdims=True)).astype(jnp.bfloat16)
    out = jnp.einsum("bhqk,bkhd->bqhd", weights, vb, preferred_element_type=jnp.float32)
    return out.reshape(row_count, head_count, head_size)


def mix_request(projected, cache_rows, length, tap_table, window, head_size):
    row_count, feat_width = (projected.shape[0], projected.shape[2])
    time_order = (length + jnp.arange(window, dtype=jnp.int32)) % window
    earlier = cache_rows[:, time_order]
    key_rows = jnp.concatenate([earlier[0], projected[:, 1]], axis=0)
    value_rows = jnp.concatenate([earlier[1], projected[:, 2]], axis=0)
    head_count = feat_width // head_size
    attended = window_attend(
        projected[:, 0].reshape(row_count, head_count, head_size),
        key_rows.reshape(-1, head_count, head_size),
        value_rows.reshape(-1, head_count, head_size),
        length,
        window,
    ).reshape(row_count, feat_width)
    positions = jnp.arange(window + row_count, dtype=jnp.int32)
    alive_mask = (positions >= window - length)[:, None]
    masked_values = jnp.where(alive_mask, value_rows.astype(jnp.float32), jnp.float32(0.0))
    tap_count = tap_table.shape[0]
    convolved = jnp.zeros((row_count, feat_width), jnp.float32)
    for tap_index in range(tap_count):
        begin_row = window - (tap_count - 1) + tap_index
        convolved = (
            convolved + tap_table[tap_index] * masked_values[begin_row : begin_row + row_count]
        )
    mixed_heads = (attended + projected[:, 3].astype(jnp.float32) * convolved).astype(jnp.bfloat16)
    slot_source = (
        row_count - window + (jnp.arange(window, dtype=jnp.int32) - length - row_count) % window
    )
    renewed = jnp.stack([projected[:, 1], projected[:, 2]])[:, slot_source]
    return (mixed_heads, renewed)


def gather_packed(pieces):
    widths = [p.shape[1] for p in pieces]
    got = lax.all_gather(jnp.concatenate(pieces, axis=1), "req", axis=0, tiled=True)
    parts = []
    start = 0
    for w in widths:
        parts.append(got[:, start : start + w])
        start += w
    return parts


def core_swap(x):
    return lax.ppermute(x, "tpc", [(0, 1), (1, 0)])


def mlp_rows(rows, ffn_all, down_t, ffn_width):
    gate_up = jnp.dot(rows, ffn_all, preferred_element_type=jnp.float32)
    activated = (jax.nn.silu(gate_up[:, :ffn_width]) * gate_up[:, ffn_width:]).astype(jnp.bfloat16)
    out = lax.dot_general(
        activated, down_t, (((1,), (1,)), ((), ())), preferred_element_type=jnp.float32
    )
    return out.astype(jnp.bfloat16)


def local(
    tokens,
    norm_gain,
    ffn_gain,
    mix_weight,
    out_weight,
    ffn_weight,
    down_weight,
    conv_taps,
    past_cache,
    cached_len,
):
    feat_width = mix_weight.shape[2]
    ffn_width = ffn_weight.shape[2]
    rows = mix_weight.shape[0]
    mix_all, out_t = gather_packed([mix_weight.reshape(rows, -1), out_weight.T])
    ffn_all, down_t = gather_packed([ffn_weight.reshape(rows, -1), down_weight.T])
    nxt = lax.axis_size("tpx")
    tok_mine = lax.all_to_all(
        jnp.tile(normed(tokens, norm_gain)[None], (nxt, 1, 1)), "tpx", 0, 0, tiled=True
    )
    tok_theirs = core_swap(tok_mine)
    first = lax.axis_index("tpc") == 0
    pairs = jnp.stack(
        [jnp.where(first, tok_mine, tok_theirs), jnp.where(first, tok_theirs, tok_mine)], axis=1
    )
    normed_all = pairs.reshape((-1,) + tok_mine.shape[2:])
    row_total = normed_all.shape[0]
    projected = jnp.dot(normed_all, mix_all, preferred_element_type=jnp.float32)
    projected = projected.astype(jnp.bfloat16).reshape(row_total, 4, feat_width)
    mixed_heads, renewed = mix_request(projected, past_cache[0], cached_len[0], conv_taps, WIN, HD)
    nx = lax.axis_size("tpx")
    nc = lax.axis_size("tpc")
    me_c = lax.axis_index("tpc")
    by_core = mixed_heads.reshape(nx, nc, -1, feat_width)
    mine_rows = lax.dynamic_index_in_dim(by_core, me_c, axis=1, keepdims=False)
    their_rows = lax.dynamic_index_in_dim(by_core, 1 - me_c, axis=1, keepdims=False)

    def out_rows(r):
        return lax.dot_general(
            r.reshape(-1, feat_width), out_t, (((1,), (1,)), ((), ())),
            preferred_element_type=jnp.float32,
        ).astype(jnp.bfloat16)

    back = core_swap(out_rows(their_rows))
    pair = (out_rows(mine_rows).astype(jnp.float32) + back.astype(jnp.float32)).astype(jnp.bfloat16)
    chips = lax.all_to_all(pair.reshape((nx, -1) + pair.shape[1:]), "tpx", 0, 0, tiled=True)
    attn_part = chips.astype(jnp.float32).sum(axis=0)
    residual = (tokens.astype(jnp.float32) + attn_part).astype(jnp.bfloat16)
    nx = lax.axis_size("tpx")
    mine = lax.all_to_all(
        jnp.tile(normed(residual, ffn_gain)[None], (nx, 1, 1)), "tpx", 0, 0, tiled=True
    )
    flat = mine.reshape((-1,) + mine.shape[2:])
    theirs = core_swap(flat)
    part_mine = mlp_rows(flat, ffn_all, down_t, ffn_width)
    part_theirs = mlp_rows(theirs, ffn_all, down_t, ffn_width)
    back = core_swap(part_theirs)
    pair = (part_mine.astype(jnp.float32) + back.astype(jnp.float32)).astype(jnp.bfloat16)
    ffn_part = lax.psum_scatter(pair, "tpx", scatter_dimension=0, tiled=True).astype(jnp.float32)
    layer_out = (residual.astype(jnp.float32) + ffn_part).astype(jnp.bfloat16)
    return (layer_out, renewed[None])


def solution(mesh):
    n_req, n_tp = mesh.devices.shape
    split = jax.sharding.Mesh(mesh.devices.reshape(n_req, n_tp // 2, 2), ("req", "tpx", "tpc"))
    tp = ("tpx", "tpc")
    in_specs = (
        P(("req",) + tp, None),
        P(),
        P(),
        P("req", None, tp),
        P(tp, "req"),
        P("req", None, tp),
        P(tp, "req"),
        P(None, tp),
        P("req", None, None, tp),
        P("req"),
    )
    out_specs = (P(("req",) + tp, None), P("req", None, None, tp))
    return jax.shard_map(local, mesh=split, in_specs=in_specs, out_specs=out_specs, check_vma=False)
```

```python
import math

import jax
import jax.numpy as jnp
from jax import lax
from jax.sharding import PartitionSpec as P

HD = 112
WIN = 64


def normed(row_vals, gain):
    floats = row_vals.astype(jnp.float32)
    scaled = floats * lax.rsqrt(jnp.mean(floats * floats, axis=-1, keepdims=True) + 1e-05)
    return (scaled * gain).astype(jnp.bfloat16)


def window_attend(queries, key_rows, value_rows, length, window):
    row_count, head_count, head_size = queries.shape
    nb = row_count // window
    score_scale = 1.0 / math.sqrt(head_size)
    qb = queries.reshape(nb, window, head_count, head_size)

    def blocks(rows):
        lo = rows[:row_count].reshape(nb, window, head_count, head_size)
        hi = rows[window:].reshape(nb, window, head_count, head_size)
        return jnp.concatenate([lo, hi], axis=1)

    kb = blocks(key_rows)
    vb = blocks(value_rows)
    scores = (
        jnp.einsum("bqhd,bkhd->bhqk", qb, kb, preferred_element_type=jnp.float32) * score_scale
    )
    i = jnp.arange(window, dtype=jnp.int32)[:, None]
    j = jnp.arange(2 * window, dtype=jnp.int32)[None, :]
    b = jnp.arange(nb, dtype=jnp.int32)[:, None, None]
    usable = (j > i)[None] & (j <= i + window)[None] & (b * window + j >= window - length)
    scores = jnp.where(usable[:, None], scores, -1e30)
    row_max = jnp.max(scores, axis=-1, keepdims=True)
    exponent = jnp.exp(scores - row_max)
    weights = (exponent / jnp.sum(exponent, axis=-1, keepdims=True)).astype(jnp.bfloat16)
    out = jnp.einsum("bhqk,bkhd->bqhd", weights, vb, preferred_element_type=jnp.float32)
    return out.reshape(row_count, head_count, head_size)


def mix_request(projected, cache_rows, length, tap_table, window, head_size):
    row_count, feat_width = (projected.shape[0], projected.shape[2])
    time_order = (length + jnp.arange(window, dtype=jnp.int32)) % window
    earlier = cache_rows[:, time_order]
    key_rows = jnp.concatenate([earlier[0], projected[:, 1]], axis=0)
    value_rows = jnp.concatenate([earlier[1], projected[:, 2]], axis=0)
    head_count = feat_width // head_size
    attended = window_attend(
        projected[:, 0].reshape(row_count, head_count, head_size),
        key_rows.reshape(-1, head_count, head_size),
        value_rows.reshape(-1, head_count, head_size),
        length,
        window,
    ).reshape(row_count, feat_width)
    positions = jnp.arange(window + row_count, dtype=jnp.int32)
    alive_mask = (positions >= window - length)[:, None]
    masked_values = jnp.where(alive_mask, value_rows.astype(jnp.float32), jnp.float32(0.0))
    tap_count = tap_table.shape[0]
    convolved = jnp.zeros((row_count, feat_width), jnp.float32)
    for tap_index in range(tap_count):
        begin_row = window - (tap_count - 1) + tap_index
        convolved = (
            convolved + tap_table[tap_index] * masked_values[begin_row : begin_row + row_count]
        )
    mixed_heads = (attended + projected[:, 3].astype(jnp.float32) * convolved).astype(jnp.bfloat16)
    slot_source = (
        row_count - window + (jnp.arange(window, dtype=jnp.int32) - length - row_count) % window
    )
    renewed = jnp.stack([projected[:, 1], projected[:, 2]])[:, slot_source]
    return (mixed_heads, renewed)


def gather_packed(pieces):
    widths = [p.shape[1] for p in pieces]
    got = lax.all_gather(jnp.concatenate(pieces, axis=1), "req", axis=0, tiled=True)
    parts = []
    start = 0
    for w in widths:
        parts.append(got[:, start : start + w])
        start += w
    return parts


def core_swap(x):
    return lax.ppermute(x, "tpc", [(0, 1), (1, 0)])


def ring_pass(x, axis, step):
    n = lax.axis_size(axis)
    return lax.ppermute(x, axis, [(i, (i + step) % n) for i in range(n)])


def ring_sum_scatter(chunk):
    far = chunk(2)
    half = far.shape[-1] // 2
    far_a = ring_pass(ring_pass(far[:, :half], "tpx", 1), "tpx", 1)
    far_b = ring_pass(ring_pass(far[:, half:], "tpx", -1), "tpx", -1)
    from_left = ring_pass(chunk(1), "tpx", 1)
    from_right = ring_pass(chunk(3), "tpx", -1)
    f32 = jnp.float32
    total = chunk(0).astype(f32) + from_left.astype(f32) + from_right.astype(f32)
    return total + jnp.concatenate([far_a, far_b], axis=-1).astype(f32)


def mlp_rows(rows, ffn_all, down_t, ffn_width):
    gate_up = jnp.dot(rows, ffn_all, preferred_element_type=jnp.float32)
    activated = (jax.nn.silu(gate_up[:, :ffn_width]) * gate_up[:, ffn_width:]).astype(jnp.bfloat16)
    out = lax.dot_general(
        activated, down_t, (((1,), (1,)), ((), ())), preferred_element_type=jnp.float32
    )
    return out.astype(jnp.bfloat16)


def local(
    tokens,
    norm_gain,
    ffn_gain,
    mix_weight,
    out_weight,
    ffn_weight,
    down_weight,
    conv_taps,
    past_cache,
    cached_len,
):
    feat_width = mix_weight.shape[2]
    ffn_width = ffn_weight.shape[2]
    rows = mix_weight.shape[0]
    mix_all, out_t = gather_packed([mix_weight.reshape(rows, -1), out_weight.T])
    ffn_all, down_t = gather_packed([ffn_weight.reshape(rows, -1), down_weight.T])
    nxt = lax.axis_size("tpx")
    tok_mine = lax.all_to_all(
        jnp.tile(normed(tokens, norm_gain)[None], (nxt, 1, 1)), "tpx", 0, 0, tiled=True
    )
    tok_theirs = core_swap(tok_mine)
    first = lax.axis_index("tpc") == 0
    pairs = jnp.stack(
        [jnp.where(first, tok_mine, tok_theirs), jnp.where(first, tok_theirs, tok_mine)], axis=1
    )
    normed_all = pairs.reshape((-1,) + tok_mine.shape[2:])
    row_total = normed_all.shape[0]
    projected = jnp.dot(normed_all, mix_all, preferred_element_type=jnp.float32)
    projected = projected.astype(jnp.bfloat16).reshape(row_total, 4, feat_width)
    mixed_heads, renewed = mix_request(projected, past_cache[0], cached_len[0], conv_taps, WIN, HD)
    nx = lax.axis_size("tpx")
    nc = lax.axis_size("tpc")
    me_c = lax.axis_index("tpc")
    by_core = mixed_heads.reshape(nx, nc, -1, feat_width)
    mine_rows = lax.dynamic_index_in_dim(by_core, me_c, axis=1, keepdims=False)
    their_rows = lax.dynamic_index_in_dim(by_core, 1 - me_c, axis=1, keepdims=False)

    def out_rows(r):
        return lax.dot_general(
            r.reshape(-1, feat_width), out_t, (((1,), (1,)), ((), ())),
            preferred_element_type=jnp.float32,
        ).astype(jnp.bfloat16)

    back = core_swap(out_rows(their_rows))
    pair = (out_rows(mine_rows).astype(jnp.float32) + back.astype(jnp.float32)).astype(jnp.bfloat16)
    chips = lax.all_to_all(pair.reshape((nx, -1) + pair.shape[1:]), "tpx", 0, 0, tiled=True)
    attn_part = chips.astype(jnp.float32).sum(axis=0)
    residual = (tokens.astype(jnp.float32) + attn_part).astype(jnp.bfloat16)
    nx = lax.axis_size("tpx")
    mine = lax.all_to_all(
        jnp.tile(normed(residual, ffn_gain)[None], (nx, 1, 1)), "tpx", 0, 0, tiled=True
    )
    flat = mine.reshape((-1,) + mine.shape[2:])
    theirs = core_swap(flat)
    back = core_swap(mlp_rows(theirs, ffn_all, down_t, ffn_width)).reshape(mine.shape)
    me_x = lax.axis_index("tpx")

    def chunk(k):
        dest = (me_x + k) % nx
        rows_k = lax.dynamic_index_in_dim(mine, dest, axis=0, keepdims=False)
        part = mlp_rows(rows_k, ffn_all, down_t, ffn_width).astype(jnp.float32)
        from_pair = lax.dynamic_index_in_dim(back, dest, axis=0, keepdims=False)
        return (part + from_pair.astype(jnp.float32)).astype(jnp.bfloat16)

    ffn_part = ring_sum_scatter(chunk)
    layer_out = (residual.astype(jnp.float32) + ffn_part).astype(jnp.bfloat16)
    return (layer_out, renewed[None])


def solution(mesh):
    n_req, n_tp = mesh.devices.shape
    split = jax.sharding.Mesh(mesh.devices.reshape(n_req, n_tp // 2, 2), ("req", "tpx", "tpc"))
    tp = ("tpx", "tpc")
    in_specs = (
        P(("req",) + tp, None),
        P(),
        P(),
        P("req", None, tp),
        P(tp, "req"),
        P("req", None, tp),
        P(tp, "req"),
        P(None, tp),
        P("req", None, None, tp),
        P("req"),
    )
    out_specs = (P(("req",) + tp, None), P("req", None, None, tp))
    return jax.shard_map(local, mesh=split, in_specs=in_specs, out_specs=out_specs, check_vma=False)
```

```python
import math

import jax
import jax.numpy as jnp
from jax import lax
from jax.sharding import PartitionSpec as P

HD = 112
WIN = 64


def normed(row_vals, gain):
    floats = row_vals.astype(jnp.float32)
    scaled = floats * lax.rsqrt(jnp.mean(floats * floats, axis=-1, keepdims=True) + 1e-05)
    return (scaled * gain).astype(jnp.bfloat16)


def window_attend(queries, key_rows, value_rows, length, window):
    row_count, head_count, head_size = queries.shape
    nb = row_count // window
    score_scale = 1.0 / math.sqrt(head_size)
    qb = queries.reshape(nb, window, head_count, head_size)

    def blocks(rows):
        lo = rows[:row_count].reshape(nb, window, head_count, head_size)
        hi = rows[window:].reshape(nb, window, head_count, head_size)
        return jnp.concatenate([lo, hi], axis=1)

    kb = blocks(key_rows)
    vb = blocks(value_rows)
    scores = (
        jnp.einsum("bqhd,bkhd->bhqk", qb, kb, preferred_element_type=jnp.float32) * score_scale
    )
    i = jnp.arange(window, dtype=jnp.int32)[:, None]
    j = jnp.arange(2 * window, dtype=jnp.int32)[None, :]
    b = jnp.arange(nb, dtype=jnp.int32)[:, None, None]
    usable = (j > i)[None] & (j <= i + window)[None] & (b * window + j >= window - length)
    scores = jnp.where(usable[:, None], scores, -1e30)
    row_max = jnp.max(scores, axis=-1, keepdims=True)
    exponent = jnp.exp(scores - row_max)
    weights = (exponent / jnp.sum(exponent, axis=-1, keepdims=True)).astype(jnp.bfloat16)
    out = jnp.einsum("bhqk,bkhd->bqhd", weights, vb, preferred_element_type=jnp.float32)
    return out.reshape(row_count, head_count, head_size)


def mix_request(projected, cache_rows, length, tap_table, window, head_size):
    row_count, feat_width = (projected.shape[0], projected.shape[2])
    time_order = (length + jnp.arange(window, dtype=jnp.int32)) % window
    earlier = cache_rows[:, time_order]
    key_rows = jnp.concatenate([earlier[0], projected[:, 1]], axis=0)
    value_rows = jnp.concatenate([earlier[1], projected[:, 2]], axis=0)
    head_count = feat_width // head_size
    attended = window_attend(
        projected[:, 0].reshape(row_count, head_count, head_size),
        key_rows.reshape(-1, head_count, head_size),
        value_rows.reshape(-1, head_count, head_size),
        length,
        window,
    ).reshape(row_count, feat_width)
    positions = jnp.arange(window + row_count, dtype=jnp.int32)
    alive_mask = (positions >= window - length)[:, None]
    masked_values = jnp.where(alive_mask, value_rows.astype(jnp.float32), jnp.float32(0.0))
    tap_count = tap_table.shape[0]
    convolved = jnp.zeros((row_count, feat_width), jnp.float32)
    for tap_index in range(tap_count):
        begin_row = window - (tap_count - 1) + tap_index
        convolved = (
            convolved + tap_table[tap_index] * masked_values[begin_row : begin_row + row_count]
        )
    mixed_heads = (attended + projected[:, 3].astype(jnp.float32) * convolved).astype(jnp.bfloat16)
    slot_source = (
        row_count - window + (jnp.arange(window, dtype=jnp.int32) - length - row_count) % window
    )
    renewed = jnp.stack([projected[:, 1], projected[:, 2]])[:, slot_source]
    return (mixed_heads, renewed)


def gather_packed(pieces):
    widths = [p.shape[1] for p in pieces]
    got = lax.all_gather(jnp.concatenate(pieces, axis=1), "req", axis=0, tiled=True)
    parts = []
    start = 0
    for w in widths:
        parts.append(got[:, start : start + w])
        start += w
    return parts


def core_swap(x):
    return lax.ppermute(x, "tpc", [(0, 1), (1, 0)])


def mlp_rows(rows, ffn_all, down_t, ffn_width):
    gate_up = jnp.dot(rows, ffn_all, preferred_element_type=jnp.float32)
    activated = (jax.nn.silu(gate_up[:, :ffn_width]) * gate_up[:, ffn_width:]).astype(jnp.bfloat16)
    out = lax.dot_general(
        activated, down_t, (((1,), (1,)), ((), ())), preferred_element_type=jnp.float32
    )
    return out.astype(jnp.bfloat16)


def local(
    tokens,
    norm_gain,
    ffn_gain,
    mix_weight,
    out_weight,
    ffn_weight,
    down_weight,
    conv_taps,
    past_cache,
    cached_len,
):
    feat_width = mix_weight.shape[2]
    ffn_width = ffn_weight.shape[2]
    rows = mix_weight.shape[0]
    mix_all, out_t = gather_packed([mix_weight.reshape(rows, -1), out_weight.T])
    ffn_all, down_t = gather_packed([ffn_weight.reshape(rows, -1), down_weight.T])
    nxt = lax.axis_size("tpx")
    tok_mine = lax.all_to_all(
        jnp.tile(normed(tokens, norm_gain)[None], (nxt, 1, 1)), "tpx", 0, 0, tiled=True
    )
    tok_theirs = core_swap(tok_mine)
    first = lax.axis_index("tpc") == 0
    pairs = jnp.stack(
        [jnp.where(first, tok_mine, tok_theirs), jnp.where(first, tok_theirs, tok_mine)], axis=1
    )
    normed_all = pairs.reshape((-1,) + tok_mine.shape[2:])
    row_total = normed_all.shape[0]
    projected = jnp.dot(normed_all, mix_all, preferred_element_type=jnp.float32)
    projected = projected.astype(jnp.bfloat16).reshape(row_total, 4, feat_width)
    mixed_heads, renewed = mix_request(projected, past_cache[0], cached_len[0], conv_taps, WIN, HD)
    nx = lax.axis_size("tpx")
    nc = lax.axis_size("tpc")
    me_c = lax.axis_index("tpc")
    by_core = mixed_heads.reshape(nx, nc, -1, feat_width)
    mine_rows = lax.dynamic_index_in_dim(by_core, me_c, axis=1, keepdims=False)
    their_rows = lax.dynamic_index_in_dim(by_core, 1 - me_c, axis=1, keepdims=False)

    def out_rows(r):
        return lax.dot_general(
            r.reshape(-1, feat_width), out_t, (((1,), (1,)), ((), ())),
            preferred_element_type=jnp.float32,
        ).astype(jnp.bfloat16)

    back = core_swap(out_rows(their_rows))
    pair = (out_rows(mine_rows).astype(jnp.float32) + back.astype(jnp.float32)).astype(jnp.bfloat16)
    chips = lax.all_to_all(pair.reshape((nx, -1) + pair.shape[1:]), "tpx", 0, 0, tiled=True)
    attn_part = chips.astype(jnp.float32).sum(axis=0)
    residual = (tokens.astype(jnp.float32) + attn_part).astype(jnp.bfloat16)
    nx = lax.axis_size("tpx")
    mine = lax.all_to_all(
        jnp.tile(normed(residual, ffn_gain)[None], (nx, 1, 1)), "tpx", 0, 0, tiled=True
    )
    flat = mine.reshape((-1,) + mine.shape[2:])
    theirs = core_swap(flat)
    both = jnp.concatenate([theirs, flat], axis=0)
    gate_up = jnp.dot(both, ffn_all, preferred_element_type=jnp.float32)
    activated = (jax.nn.silu(gate_up[:, :ffn_width]) * gate_up[:, ffn_width:]).astype(jnp.bfloat16)
    n_rows = flat.shape[0]

    def down_rows(a):
        return lax.dot_general(
            a, down_t, (((1,), (1,)), ((), ())), preferred_element_type=jnp.float32
        ).astype(jnp.bfloat16)

    back = core_swap(down_rows(activated[:n_rows]))
    part_mine = down_rows(activated[n_rows:])
    pair = (part_mine.astype(jnp.float32) + back.astype(jnp.float32)).astype(jnp.bfloat16)
    ffn_part = lax.psum_scatter(pair, "tpx", scatter_dimension=0, tiled=True).astype(jnp.float32)
    layer_out = (residual.astype(jnp.float32) + ffn_part).astype(jnp.bfloat16)
    return (layer_out, renewed[None])


def solution(mesh):
    n_req, n_tp = mesh.devices.shape
    split = jax.sharding.Mesh(mesh.devices.reshape(n_req, n_tp // 2, 2), ("req", "tpx", "tpc"))
    tp = ("tpx", "tpc")
    in_specs = (
        P(("req",) + tp, None),
        P(),
        P(),
        P("req", None, tp),
        P(tp, "req"),
        P("req", None, tp),
        P(tp, "req"),
        P(None, tp),
        P("req", None, None, tp),
        P("req"),
    )
    out_specs = (P(("req",) + tp, None), P("req", None, None, tp))
    return jax.shard_map(local, mesh=split, in_specs=in_specs, out_specs=out_specs, check_vma=False)
```

```python
import math

import jax
import jax.numpy as jnp
from jax import lax
from jax.sharding import PartitionSpec as P

HD = 112
WIN = 64


def normed(row_vals, gain):
    floats = row_vals.astype(jnp.float32)
    scaled = floats * lax.rsqrt(jnp.mean(floats * floats, axis=-1, keepdims=True) + 1e-05)
    return (scaled * gain).astype(jnp.bfloat16)


def window_attend(queries, key_rows, value_rows, length, window):
    row_count, head_count, head_size = queries.shape
    nb = row_count // window
    score_scale = 1.0 / math.sqrt(head_size)
    qb = queries.reshape(nb, window, head_count, head_size)

    def blocks(rows):
        lo = rows[:row_count].reshape(nb, window, head_count, head_size)
        hi = rows[window:].reshape(nb, window, head_count, head_size)
        return jnp.concatenate([lo, hi], axis=1)

    kb = blocks(key_rows)
    vb = blocks(value_rows)
    scores = (
        jnp.einsum("bqhd,bkhd->bhqk", qb, kb, preferred_element_type=jnp.float32) * score_scale
    )
    i = jnp.arange(window, dtype=jnp.int32)[:, None]
    j = jnp.arange(2 * window, dtype=jnp.int32)[None, :]
    b = jnp.arange(nb, dtype=jnp.int32)[:, None, None]
    usable = (j > i)[None] & (j <= i + window)[None] & (b * window + j >= window - length)
    scores = jnp.where(usable[:, None], scores, -1e30)
    row_max = jnp.max(scores, axis=-1, keepdims=True)
    exponent = jnp.exp(scores - row_max)
    weights = (exponent / jnp.sum(exponent, axis=-1, keepdims=True)).astype(jnp.bfloat16)
    out = jnp.einsum("bhqk,bkhd->bqhd", weights, vb, preferred_element_type=jnp.float32)
    return out.reshape(row_count, head_count, head_size)


def mix_request(projected, cache_rows, length, tap_table, window, head_size):
    row_count, feat_width = (projected.shape[0], projected.shape[2])
    time_order = (length + jnp.arange(window, dtype=jnp.int32)) % window
    earlier = cache_rows[:, time_order]
    key_rows = jnp.concatenate([earlier[0], projected[:, 1]], axis=0)
    value_rows = jnp.concatenate([earlier[1], projected[:, 2]], axis=0)
    head_count = feat_width // head_size
    attended = window_attend(
        projected[:, 0].reshape(row_count, head_count, head_size),
        key_rows.reshape(-1, head_count, head_size),
        value_rows.reshape(-1, head_count, head_size),
        length,
        window,
    ).reshape(row_count, feat_width)
    positions = jnp.arange(window + row_count, dtype=jnp.int32)
    alive_mask = (positions >= window - length)[:, None]
    masked_values = jnp.where(alive_mask, value_rows.astype(jnp.float32), jnp.float32(0.0))
    tap_count = tap_table.shape[0]
    convolved = jnp.zeros((row_count, feat_width), jnp.float32)
    for tap_index in range(tap_count):
        begin_row = window - (tap_count - 1) + tap_index
        convolved = (
            convolved + tap_table[tap_index] * masked_values[begin_row : begin_row + row_count]
        )
    mixed_heads = (attended + projected[:, 3].astype(jnp.float32) * convolved).astype(jnp.bfloat16)
    slot_source = (
        row_count - window + (jnp.arange(window, dtype=jnp.int32) - length - row_count) % window
    )
    renewed = jnp.stack([projected[:, 1], projected[:, 2]])[:, slot_source]
    return (mixed_heads, renewed)


def gather_packed(pieces):
    widths = [p.shape[1] for p in pieces]
    got = lax.all_gather(jnp.concatenate(pieces, axis=1), "req", axis=0, tiled=True)
    parts = []
    start = 0
    for w in widths:
        parts.append(got[:, start : start + w])
        start += w
    return parts


def core_swap(x):
    return lax.ppermute(x, "tpc", [(0, 1), (1, 0)])


def mlp_rows(rows, ffn_all, down_t, ffn_width):
    gate_up = jnp.dot(rows, ffn_all, preferred_element_type=jnp.float32)
    activated = (jax.nn.silu(gate_up[:, :ffn_width]) * gate_up[:, ffn_width:]).astype(jnp.bfloat16)
    out = lax.dot_general(
        activated, down_t, (((1,), (1,)), ((), ())), preferred_element_type=jnp.float32
    )
    return out.astype(jnp.bfloat16)


def local(
    tokens,
    norm_gain,
    ffn_gain,
    mix_weight,
    out_weight,
    ffn_weight,
    down_weight,
    conv_taps,
    past_cache,
    cached_len,
):
    feat_width = mix_weight.shape[2]
    ffn_width = ffn_weight.shape[2]
    rows = mix_weight.shape[0]
    mix_all, out_t = gather_packed([mix_weight.reshape(rows, -1), out_weight.T])
    ffn_all, down_t = gather_packed([ffn_weight.reshape(rows, -1), down_weight.T])
    nxt = lax.axis_size("tpx")
    tok_mine = lax.all_to_all(
        jnp.tile(normed(tokens, norm_gain)[None], (nxt, 1, 1)), "tpx", 0, 0, tiled=True
    )
    tok_theirs = core_swap(tok_mine)
    first = lax.axis_index("tpc") == 0
    pairs = jnp.stack(
        [jnp.where(first, tok_mine, tok_theirs), jnp.where(first, tok_theirs, tok_mine)], axis=1
    )
    normed_all = pairs.reshape((-1,) + tok_mine.shape[2:])
    row_total = normed_all.shape[0]
    projected = jnp.dot(normed_all, mix_all, preferred_element_type=jnp.float32)
    projected = projected.astype(jnp.bfloat16).reshape(row_total, 4, feat_width)
    mixed_heads, renewed = mix_request(projected, past_cache[0], cached_len[0], conv_taps, WIN, HD)
    nx = lax.axis_size("tpx")
    nc = lax.axis_size("tpc")
    me_c = lax.axis_index("tpc")
    by_core = mixed_heads.reshape(nx, nc, -1, feat_width)
    mine_rows = lax.dynamic_index_in_dim(by_core, me_c, axis=1, keepdims=False)
    their_rows = lax.dynamic_index_in_dim(by_core, 1 - me_c, axis=1, keepdims=False)

    def out_rows(r):
        return lax.dot_general(
            r.reshape(-1, feat_width), out_t, (((1,), (1,)), ((), ())),
            preferred_element_type=jnp.float32,
        ).astype(jnp.bfloat16)

    back = core_swap(out_rows(their_rows))
    pair = (out_rows(mine_rows).astype(jnp.float32) + back.astype(jnp.float32)).astype(jnp.bfloat16)
    chips = lax.all_to_all(pair.reshape((nx, -1) + pair.shape[1:]), "tpx", 0, 0, tiled=True)
    attn_part = chips.astype(jnp.float32).sum(axis=0)
    residual = (tokens.astype(jnp.float32) + attn_part).astype(jnp.bfloat16)
    nx = lax.axis_size("tpx")
    mine = lax.all_to_all(
        jnp.tile(normed(residual, ffn_gain)[None], (nx, 1, 1)), "tpx", 0, 0, tiled=True
    )
    flat = mine.reshape((-1,) + mine.shape[2:])
    theirs = core_swap(flat)
    part_mine = mlp_rows(flat, ffn_all, down_t, ffn_width)
    part_theirs = mlp_rows(theirs, ffn_all, down_t, ffn_width)
    back = core_swap(part_theirs)
    pair = (part_mine.astype(jnp.float32) + back.astype(jnp.float32)).astype(jnp.bfloat16)
    cols = pair.shape[1] // 2
    on_sc = lax.psum_scatter(pair[:, :cols], "tpx", scatter_dimension=0, tiled=True)
    by_a2a = lax.all_to_all(pair[:, cols:].reshape((nx, -1, cols)), "tpx", 0, 0, tiled=True)
    ffn_part = jnp.concatenate(
        [on_sc.astype(jnp.float32), by_a2a.astype(jnp.float32).sum(axis=0)], axis=1
    )
    layer_out = (residual.astype(jnp.float32) + ffn_part).astype(jnp.bfloat16)
    return (layer_out, renewed[None])


def solution(mesh):
    n_req, n_tp = mesh.devices.shape
    split = jax.sharding.Mesh(mesh.devices.reshape(n_req, n_tp // 2, 2), ("req", "tpx", "tpc"))
    tp = ("tpx", "tpc")
    in_specs = (
        P(("req",) + tp, None),
        P(),
        P(),
        P("req", None, tp),
        P(tp, "req"),
        P("req", None, tp),
        P(tp, "req"),
        P(None, tp),
        P("req", None, None, tp),
        P("req"),
    )
    out_specs = (P(("req",) + tp, None), P("req", None, None, tp))
    return jax.shard_map(local, mesh=split, in_specs=in_specs, out_specs=out_specs, check_vma=False)
```
